512 devices in a mesh: tm: 16 (over y_lo, x), space: 32 (over z, y_hi, core).
Axes of the slice: x: 4, y: 8 (y_hi: 2, y_lo: 4; y = y_hi * 4 + y_lo), z: 8, core: 2. Of those that a mesh axis runs over, the one named last changes fastest.
Arguments:
- frames: bfloat16 [16, 64, 96, 384], P('tm', 'space'), may hold values from -8 to 8
- cache_in: bfloat16 [2, 64, 96, 384], P(None, 'space'), may hold values from -6 to 6
- norm_gain: bfloat16 [384], replicated, may hold values from 0.5 to 1.5
- w_qkv: bfloat16 [384, 1152], replicated, may hold values from -0.5 to 0.5
- b_qkv: bfloat16 [1152], replicated, may hold values from -3 to 3
- w_proj: bfloat16 [384, 384], replicated, may hold values from -1.25 to 1.25
- b_proj: bfloat16 [384], replicated, may hold values from -2 to 2
- w_time: bfloat16 [3, 384, 768], replicated, may hold values from -0.1875 to 0.1875
- b_time: bfloat16 [768], replicated, may hold values from -3 to 3
- w_space: bfloat16 [3, 3, 384, 192], replicated, may hold values from -0.109375 to 0.109375
- b_space: bfloat16 [192], replicated, may hold values from -3 to 3
Outputs:
- decoded: bfloat16 [32, 128, 192, 192], P('tm', 'space')
The draws below stay inside these ranges and needn't reach their ends.
All inputs are finite; a program needn't handle non-finite values.
Results may differ from the reference program's by a relative error of at most 0.01.
Values may be sent and summed in bfloat16 or wider, within the bound.
No kernel may reach another device: no remote copies, remote signals or barrier semaphores. Data moves between devices by JAX's collectives and lax.ppermute only.
A program may use at most 64 MiB of HBM per device.

```python
import jax
import jax.numpy as jnp
from jax import lax

C = 384
C2 = 192
COLS = 96
FRAMES = 16
HEIGHT = 64


def draw_frames(key, part):
    shape = (FRAMES, HEIGHT, COLS, C)
    base = jnp.clip(jax.random.normal(jax.random.fold_in(key, 1), shape, jnp.float32), -6.0, 6.0)
    return base.astype(jnp.bfloat16)


def draw_w_qkv(key, part):
    column = jnp.arange(3 * C)
    raw = jax.random.normal(jax.random.fold_in(key, 4), (C, 3 * C), jnp.float32) * C ** (-0.5)
    raw = raw * jnp.where(column < 2 * C, 1.7, 1.0)
    raw = jnp.clip(raw, -0.45, 0.45)
    return raw.astype(jnp.bfloat16)


def levels(key, extent, pieces, smallest, largest):
    loudness = 1.0
    for position, shards_of in pieces:
        draws = jax.random.uniform(jax.random.fold_in(jax.random.fold_in(key, 6), position), (shards_of,), jnp.float32, smallest / len(pieces), largest / len(pieces))
        loudness = loudness * jnp.repeat(jnp.exp(draws), extent[position] // shards_of).reshape((-1,) + (1,) * (len(extent) - 1 - position))
    return loudness


def normal_values(rng, dims, scale, reach, cuts=(), held_as=jnp.bfloat16):
    array = scale * jax.random.normal(rng, dims, jnp.float32)
    if cuts:
        array = array * levels(rng, dims, cuts, -0.22, 0.18)
    return jnp.clip(array, -reach, reach).astype(held_as)


def setup_inputs(seed: int = 0) -> dict:
    key_list = jax.random.split(jax.random.key(seed), 12)
    return {
        "frames": draw_frames(jax.random.fold_in(key_list[11], 71), 0),
        "cache_in": normal_values(key_list[1], (2, HEIGHT, COLS, C), 1.0, 6.0, ((1, 32),)),
        "norm_gain": jnp.clip(1.0 + 0.1 * jax.random.normal(key_list[2], (C,), jnp.float32), 0.5, 1.5).astype(jnp.bfloat16),
        "w_qkv": draw_w_qkv(jax.random.fold_in(key_list[11], 71), 0),
        "b_qkv": normal_values(key_list[4], (3 * C,), 0.5, 3.0),
        "w_proj": normal_values(key_list[5], (C, C), (C // 16) ** -0.5, 1.25),
        "b_proj": normal_values(key_list[6], (C,), 0.3, 2.0),
        "w_time": normal_values(key_list[7], (3, C, 2 * C), (3 * C) ** -0.5, 0.1875),
        "b_time": normal_values(key_list[8], (2 * C,), 0.5, 3.0),
        "w_space": normal_values(key_list[9], (3, 3, C, C2), (9 * C) ** -0.5, 0.109375),
        "b_space": normal_values(key_list[10], (C2,), 0.5, 3.0),
    }


EPSILON = 1e-06

def normalize(frames, norm_gain):
    widened = frames.astype(jnp.float32)
    inverse = lax.rsqrt(lax.optimization_barrier(jnp.mean(widened * widened, axis=-1, keepdims=True)) + EPSILON)
    return (widened * inverse * norm_gain.astype(jnp.float32)).astype(jnp.bfloat16)

def project(rows, weight, bias):
    return (jnp.dot(rows, weight, preferred_element_type=jnp.float32) + bias.astype(jnp.float32)).astype(jnp.bfloat16)

def reference(frames, cache_in, norm_gain, w_qkv, b_qkv, w_proj, b_proj, w_time, b_time, w_space, b_space):
    frame_count, height, width, channels = frames.shape
    normed = normalize(frames, norm_gain).reshape(frame_count, height * width, channels)

    def frame_attention(rows):
        queries = project(rows, w_qkv[:, :channels], b_qkv[:channels])
        key_rows = project(rows, w_qkv[:, channels:2 * channels], b_qkv[channels:2 * channels])
        value_rows = project(rows, w_qkv[:, 2 * channels:], b_qkv[2 * channels:])
        scores = jnp.dot(queries, key_rows.T, preferred_element_type=jnp.float32) * channels ** (-0.5)
        row_max = lax.optimization_barrier(jnp.max(scores, axis=1, keepdims=True))
        weights = jnp.exp(scores - row_max)
        mass = lax.optimization_barrier(jnp.sum(weights, axis=1, keepdims=True))
        return (jnp.dot(weights.astype(jnp.bfloat16), value_rows, preferred_element_type=jnp.float32) / mass).astype(jnp.bfloat16)
    mixed = lax.map(frame_attention, normed).reshape(-1, channels)
    hidden = (frames.reshape(-1, channels).astype(jnp.float32) + jnp.dot(mixed, w_proj, preferred_element_type=jnp.float32) + b_proj.astype(jnp.float32)).astype(jnp.bfloat16)
    hidden = hidden.reshape(frame_count, height * width, channels)
    shifted = jnp.concatenate([cache_in.reshape(2, height * width, channels), hidden], axis=0)
    timed = jnp.zeros((frame_count * height * width, 2 * channels), jnp.float32) + b_time.astype(jnp.float32)
    for offset in range(3):
        timed = timed + jnp.dot(shifted[offset:offset + frame_count].reshape(-1, channels), w_time[offset], preferred_element_type=jnp.float32)
    timed = timed.astype(jnp.bfloat16).reshape(frame_count, height, width, 2 * channels)
    paired = jnp.stack([timed[..., :channels], timed[..., channels:]], axis=1).reshape(2 * frame_count, height, width, channels)

    def spatial(frame):
        upsampled = jnp.repeat(jnp.repeat(frame, 2, axis=0), 2, axis=1)
        padded = jnp.pad(upsampled, ((1, 1), (1, 1), (0, 0)))
        result = jnp.zeros((4 * height * width, w_space.shape[-1]), jnp.float32) + b_space.astype(jnp.float32)
        for row_tap in range(3):
            for col_tap in range(3):
                window = padded[row_tap:row_tap + 2 * height, col_tap:col_tap + 2 * width].reshape(-1, channels)
                result = result + jnp.dot(window, w_space[row_tap, col_tap], preferred_element_type=jnp.float32)
        return result.astype(jnp.bfloat16).reshape(2 * height, 2 * width, w_space.shape[-1])
    return lax.map(spatial, paired)
```

```python
import jax
import jax.numpy as jnp
from jax import lax
from jax.sharding import PartitionSpec as P

EPSILON = 1e-06


def shifted(value, axis, steps):
    count = lax.axis_size(axis)
    leading, last = (max(0, -steps), min(count, count - steps))
    return lax.ppermute(value, axis, [(source, source + steps) for source in range(leading, last)])


def with_halo(block, sides, width):
    for axis, dim in sides:
        count = lax.axis_size(axis)
        forward = [(i, i + 1) for i in range(count - 1)]
        backward = [(target, source) for source, target in forward]
        low = lax.ppermute(
            lax.slice_in_dim(block, block.shape[dim] - width, None, axis=dim), axis, forward
        )
        high = lax.ppermute(lax.slice_in_dim(block, 0, width, axis=dim), axis, backward)
        block = jnp.concatenate([low, block, high], axis=dim)
    return block


def normalize(frames, norm_gain):
    widened = frames.astype(jnp.float32)
    inverse = lax.rsqrt(jnp.mean(widened * widened, axis=-1, keepdims=True) + EPSILON)
    return (widened * inverse * norm_gain.astype(jnp.float32)).astype(jnp.bfloat16)


def project(rows, weight, bias):
    return (
        jnp.dot(rows, weight, preferred_element_type=jnp.float32) + bias.astype(jnp.float32)
    ).astype(jnp.bfloat16)


def attend(running, queries, key_rows, value_rows):
    best, mass, total_sum = running
    scores = lax.dot_general(
        queries, key_rows, (((1,), (1,)), ((), ())), preferred_element_type=jnp.float32
    ) * queries.shape[1] ** (-0.5)
    new_best = jnp.maximum(best, jnp.max(scores, axis=1, keepdims=True))
    weights = jnp.exp(scores - new_best)
    mass = jnp.sum(weights, axis=1, keepdims=True)
    total_sum = jnp.dot(
        weights.astype(jnp.bfloat16), value_rows, preferred_element_type=jnp.float32
    )
    return (new_best, mass, total_sum)


def body(
    frames, cache_in, norm_gain, w_qkv, b_qkv, w_proj, b_proj, w_time, b_time, w_space, b_space
):
    channels = frames.shape[-1]
    rows = frames.shape[1]
    width = frames.shape[2]
    whole = lax.all_gather(frames.reshape(-1, channels), "space", axis=0, tiled=True)
    normed = normalize(frames, norm_gain).reshape(-1, channels)
    queries = project(normed, w_qkv[:, :channels], b_qkv[:channels])
    count = queries.shape[0]
    start_state = (
        jnp.full((count, 1), -1e30, jnp.float32),
        jnp.zeros((count, 1), jnp.float32),
        jnp.zeros((count, channels), jnp.float32),
    )
    normed_all = normalize(whole, norm_gain)
    key_rows = project(normed_all, w_qkv[:, channels : 2 * channels], b_qkv[channels : 2 * channels])
    value_rows = project(normed_all, w_qkv[:, 2 * channels :], b_qkv[2 * channels :])
    final = attend(start_state, queries, key_rows, value_rows)
    mixed = (final[2] / final[1]).astype(jnp.bfloat16)
    hidden = (
        frames.reshape(-1, channels).astype(jnp.float32)
        + jnp.dot(mixed, w_proj, preferred_element_type=jnp.float32)
        + b_proj.astype(jnp.float32)
    ).astype(jnp.bfloat16)
    position = lax.axis_index("tm")
    carried = cache_in.reshape(2, -1, channels)
    near_frame = shifted(hidden, "tm", 1)
    near_frame = jnp.where(position == 0, carried[1], near_frame)
    far_frame = shifted(hidden, "tm", 2)
    far_frame = jnp.where(position == 1, carried[1], far_frame)
    far_frame = jnp.where(position == 0, carried[0], far_frame)
    timed = b_time.astype(jnp.float32) + jnp.dot(
        far_frame, w_time[0], preferred_element_type=jnp.float32
    )
    timed = timed + jnp.dot(near_frame, w_time[1], preferred_element_type=jnp.float32)
    timed = (timed + jnp.dot(hidden, w_time[2], preferred_element_type=jnp.float32)).astype(
        jnp.bfloat16
    )
    paired = jnp.stack([timed[:, :channels], timed[:, channels:]]).reshape(2, rows, width, channels)
    padded = with_halo(paired, (("space", 1),), 1)
    upsampled = jnp.repeat(jnp.repeat(padded, 2, axis=1)[:, 1 : 2 * rows + 3], 2, axis=2)
    upsampled = jnp.pad(upsampled, ((0, 0), (0, 0), (1, 1), (0, 0)))
    out_channels = w_space.shape[-1]
    result = jnp.zeros((8 * rows * width, out_channels), jnp.float32) + b_space.astype(jnp.float32)
    for row_tap in range(3):
        for col_tap in range(3):
            window = upsampled[
                :, row_tap : row_tap + 2 * rows, col_tap : col_tap + 2 * width
            ].reshape(-1, channels)
            result = result + jnp.dot(
                window, w_space[row_tap, col_tap], preferred_element_type=jnp.float32
            )
    return result.astype(jnp.bfloat16).reshape(2, 2 * rows, 2 * width, out_channels)


def solution(mesh):
    return jax.shard_map(
        body,
        mesh=mesh,
        in_specs=(
            P("tm", "space", None, None),
            P(None, "space", None, None),
            P(),
            P(),
            P(),
            P(),
            P(),
            P(),
            P(),
            P(),
            P(),
        ),
        out_specs=P("tm", "space", None, None),
        check_vma=False,
    )
```

```python
import jax
import jax.numpy as jnp
from jax import lax
from jax.sharding import PartitionSpec as P

EPSILON = 1e-06


def shifted(value, axis, steps):
    count = lax.axis_size(axis)
    leading, last = (max(0, -steps), min(count, count - steps))
    return lax.ppermute(value, axis, [(source, source + steps) for source in range(leading, last)])


def with_halo(block, sides, width):
    for axis, dim in sides:
        count = lax.axis_size(axis)
        forward = [(i, i + 1) for i in range(count - 1)]
        backward = [(target, source) for source, target in forward]
        low = lax.ppermute(
            lax.slice_in_dim(block, block.shape[dim] - width, None, axis=dim), axis, forward
        )
        high = lax.ppermute(lax.slice_in_dim(block, 0, width, axis=dim), axis, backward)
        block = jnp.concatenate([low, block, high], axis=dim)
    return block


def gather_space(block):
    count = lax.axis_size("space")
    rings = count // 4

    def moved(value, target):
        return lax.ppermute(value, "space", [(s, target(s)) for s in range(count)])

    partner = moved(block, lambda s: s ^ 2)
    own = jnp.concatenate([block, partner], axis=0)
    forward = lambda s: ((s // 4 + 1) % rings) * 4 + s % 4
    backward = lambda s: ((s // 4 - 1) % rings) * 4 + s % 4
    pieces = [own]
    ahead, behind = own, own
    for _ in range(rings // 2 - 1):
        ahead = moved(ahead, forward)
        behind = moved(behind, backward)
        pieces += [ahead, behind]
    half = own.shape[0] // 2
    pieces.append(moved(ahead[:half], forward))
    pieces.append(moved(behind[half:], backward))
    mine = jnp.concatenate(pieces, axis=0)
    other = [moved(piece, lambda s: s ^ 1) for piece in pieces]
    return jnp.concatenate([mine] + other, axis=0)


def normalize(frames, norm_gain):
    widened = frames.astype(jnp.float32)
    inverse = lax.rsqrt(jnp.mean(widened * widened, axis=-1, keepdims=True) + EPSILON)
    return (widened * inverse * norm_gain.astype(jnp.float32)).astype(jnp.bfloat16)


def project(rows, weight, bias):
    return (
        jnp.dot(rows, weight, preferred_element_type=jnp.float32) + bias.astype(jnp.float32)
    ).astype(jnp.bfloat16)


def attend(running, queries, key_rows, value_rows):
    best, mass, total_sum = running
    scores = lax.dot_general(
        queries, key_rows, (((1,), (1,)), ((), ())), preferred_element_type=jnp.float32
    ) * queries.shape[1] ** (-0.5)
    new_best = jnp.maximum(best, jnp.max(scores, axis=1, keepdims=True))
    weights = jnp.exp(scores - new_best)
    mass = jnp.sum(weights, axis=1, keepdims=True)
    total_sum = jnp.dot(
        weights.astype(jnp.bfloat16), value_rows, preferred_element_type=jnp.float32
    )
    return (new_best, mass, total_sum)


def body(
    frames, cache_in, norm_gain, w_qkv, b_qkv, w_proj, b_proj, w_time, b_time, w_space, b_space
):
    channels = frames.shape[-1]
    rows = frames.shape[1]
    width = frames.shape[2]
    whole = gather_space(frames.reshape(-1, channels))
    normed = normalize(frames, norm_gain).reshape(-1, channels)
    queries = project(normed, w_qkv[:, :channels], b_qkv[:channels])
    count = queries.shape[0]
    start_state = (
        jnp.full((count, 1), -1e30, jnp.float32),
        jnp.zeros((count, 1), jnp.float32),
        jnp.zeros((count, channels), jnp.float32),
    )
    normed_all = normalize(whole, norm_gain)
    key_rows = project(normed_all, w_qkv[:, channels : 2 * channels], b_qkv[channels : 2 * channels])
    value_rows = project(normed_all, w_qkv[:, 2 * channels :], b_qkv[2 * channels :])
    final = attend(start_state, queries, key_rows, value_rows)
    mixed = (final[2] / final[1]).astype(jnp.bfloat16)
    hidden = (
        frames.reshape(-1, channels).astype(jnp.float32)
        + jnp.dot(mixed, w_proj, preferred_element_type=jnp.float32)
        + b_proj.astype(jnp.float32)
    ).astype(jnp.bfloat16)
    position = lax.axis_index("tm")
    carried = cache_in.reshape(2, -1, channels)
    near_frame = shifted(hidden, "tm", 1)
    near_frame = jnp.where(position == 0, carried[1], near_frame)
    far_frame = shifted(hidden, "tm", 2)
    far_frame = jnp.where(position == 1, carried[1], far_frame)
    far_frame = jnp.where(position == 0, carried[0], far_frame)
    timed = b_time.astype(jnp.float32) + jnp.dot(
        far_frame, w_time[0], preferred_element_type=jnp.float32
    )
    timed = timed + jnp.dot(near_frame, w_time[1], preferred_element_type=jnp.float32)
    timed = (timed + jnp.dot(hidden, w_time[2], preferred_element_type=jnp.float32)).astype(
        jnp.bfloat16
    )
    paired = jnp.stack([timed[:, :channels], timed[:, channels:]]).reshape(2, rows, width, channels)
    padded = with_halo(paired, (("space", 1),), 1)
    upsampled = jnp.repeat(jnp.repeat(padded, 2, axis=1)[:, 1 : 2 * rows + 3], 2, axis=2)
    upsampled = jnp.pad(upsampled, ((0, 0), (0, 0), (1, 1), (0, 0)))
    out_channels = w_space.shape[-1]
    result = jnp.zeros((8 * rows * width, out_channels), jnp.float32) + b_space.astype(jnp.float32)
    for row_tap in range(3):
        for col_tap in range(3):
            window = upsampled[
                :, row_tap : row_tap + 2 * rows, col_tap : col_tap + 2 * width
            ].reshape(-1, channels)
            result = result + jnp.dot(
                window, w_space[row_tap, col_tap], preferred_element_type=jnp.float32
            )
    return result.astype(jnp.bfloat16).reshape(2, 2 * rows, 2 * width, out_channels)


def solution(mesh):
    return jax.shard_map(
        body,
        mesh=mesh,
        in_specs=(
            P("tm", "space", None, None),
            P(None, "space", None, None),
            P(),
            P(),
            P(),
            P(),
            P(),
            P(),
            P(),
            P(),
            P(),
        ),
        out_specs=P("tm", "space", None, None),
        check_vma=False,
    )
```

```python
import jax
import jax.numpy as jnp
from jax import lax
from jax.sharding import PartitionSpec as P

EPSILON = 1e-06


def shifted(value, axis, steps):
    count = lax.axis_size(axis)
    leading, last = (max(0, -steps), min(count, count - steps))
    return lax.ppermute(value, axis, [(source, source + steps) for source in range(leading, last)])


def with_halo(block, sides, width):
    for axis, dim in sides:
        count = lax.axis_size(axis)
        forward = [(i, i + 1) for i in range(count - 1)]
        backward = [(target, source) for source, target in forward]
        low = lax.ppermute(
            lax.slice_in_dim(block, block.shape[dim] - width, None, axis=dim), axis, forward
        )
        high = lax.ppermute(lax.slice_in_dim(block, 0, width, axis=dim), axis, backward)
        block = jnp.concatenate([low, block, high], axis=dim)
    return block


def gather_space(block):
    count = lax.axis_size("space")
    rings = count // 4

    def moved(value, target):
        return lax.ppermute(value, "space", [(s, target(s)) for s in range(count)])

    partner = moved(block, lambda s: s ^ 2)
    own = jnp.concatenate([block, partner], axis=0)
    forward = lambda s: ((s // 4 + 1) % rings) * 4 + s % 4
    backward = lambda s: ((s // 4 - 1) % rings) * 4 + s % 4
    batches = [[own]]
    ahead, behind = own, own
    for step in range(rings // 2 - 1):
        ahead = moved(ahead, forward)
        behind = moved(behind, backward)
        batches[-1] += [ahead, behind]
        if step == 0:
            batches.append([])
    half = own.shape[0] // 2
    batches[-1].append(moved(ahead[:half], forward))
    batches[-1].append(moved(behind[half:], backward))
    mine = [jnp.concatenate(batch, axis=0) for batch in batches]
    other = [moved(chunk, lambda s: s ^ 1) for chunk in mine]
    return mine + other


def normalize(frames, norm_gain):
    widened = frames.astype(jnp.float32)
    inverse = lax.rsqrt(jnp.mean(widened * widened, axis=-1, keepdims=True) + EPSILON)
    return (widened * inverse * norm_gain.astype(jnp.float32)).astype(jnp.bfloat16)


def project(rows, weight, bias):
    return (
        jnp.dot(rows, weight, preferred_element_type=jnp.float32) + bias.astype(jnp.float32)
    ).astype(jnp.bfloat16)


def attend(running, queries, key_rows, value_rows):
    best, mass, total_sum = running
    scores = lax.dot_general(
        queries, key_rows, (((1,), (1,)), ((), ())), preferred_element_type=jnp.float32
    ) * queries.shape[1] ** (-0.5)
    new_best = jnp.maximum(best, jnp.max(scores, axis=1, keepdims=True))
    correction = jnp.exp(best - new_best)
    weights = jnp.exp(scores - new_best)
    mass = mass * correction + jnp.sum(weights, axis=1, keepdims=True)
    total_sum = total_sum * correction + jnp.dot(
        weights.astype(jnp.bfloat16), value_rows, preferred_element_type=jnp.float32
    )
    return (new_best, mass, total_sum)


def body(
    frames, cache_in, norm_gain, w_qkv, b_qkv, w_proj, b_proj, w_time, b_time, w_space, b_space
):
    channels = frames.shape[-1]
    rows = frames.shape[1]
    width = frames.shape[2]
    chunks = gather_space(frames.reshape(-1, channels))
    normed = normalize(frames, norm_gain).reshape(-1, channels)
    queries = project(normed, w_qkv[:, :channels], b_qkv[:channels])
    count = queries.shape[0]
    final = (
        jnp.full((count, 1), -jnp.inf, jnp.float32),
        jnp.zeros((count, 1), jnp.float32),
        jnp.zeros((count, channels), jnp.float32),
    )
    for chunk in chunks:
        normed_chunk = normalize(chunk, norm_gain)
        key_rows = project(normed_chunk, w_qkv[:, channels : 2 * channels], b_qkv[channels : 2 * channels])
        value_rows = project(normed_chunk, w_qkv[:, 2 * channels :], b_qkv[2 * channels :])
        final = attend(final, queries, key_rows, value_rows)
    mixed = (final[2] / final[1]).astype(jnp.bfloat16)
    hidden = (
        frames.reshape(-1, channels).astype(jnp.float32)
        + jnp.dot(mixed, w_proj, preferred_element_type=jnp.float32)
        + b_proj.astype(jnp.float32)
    ).astype(jnp.bfloat16)
    position = lax.axis_index("tm")
    carried = cache_in.reshape(2, -1, channels)
    near_frame = shifted(hidden, "tm", 1)
    near_frame = jnp.where(position == 0, carried[1], near_frame)
    far_frame = shifted(hidden, "tm", 2)
    far_frame = jnp.where(position == 1, carried[1], far_frame)
    far_frame = jnp.where(position == 0, carried[0], far_frame)
    timed = b_time.astype(jnp.float32) + jnp.dot(
        far_frame, w_time[0], preferred_element_type=jnp.float32
    )
    timed = timed + jnp.dot(near_frame, w_time[1], preferred_element_type=jnp.float32)
    timed = (timed + jnp.dot(hidden, w_time[2], preferred_element_type=jnp.float32)).astype(
        jnp.bfloat16
    )
    paired = jnp.stack([timed[:, :channels], timed[:, channels:]]).reshape(2, rows, width, channels)
    padded = with_halo(paired, (("space", 1),), 1)
    upsampled = jnp.repeat(jnp.repeat(padded, 2, axis=1)[:, 1 : 2 * rows + 3], 2, axis=2)
    upsampled = jnp.pad(upsampled, ((0, 0), (0, 0), (1, 1), (0, 0)))
    out_channels = w_space.shape[-1]
    result = jnp.zeros((8 * rows * width, out_channels), jnp.float32) + b_space.astype(jnp.float32)
    for row_tap in range(3):
        for col_tap in range(3):
            window = upsampled[
                :, row_tap : row_tap + 2 * rows, col_tap : col_tap + 2 * width
            ].reshape(-1, channels)
            result = result + jnp.dot(
                window, w_space[row_tap, col_tap], preferred_element_type=jnp.float32
            )
    return result.astype(jnp.bfloat16).reshape(2, 2 * rows, 2 * width, out_channels)


def solution(mesh):
    return jax.shard_map(
        body,
        mesh=mesh,
        in_specs=(
            P("tm", "space", None, None),
            P(None, "space", None, None),
            P(),
            P(),
            P(),
            P(),
            P(),
            P(),
            P(),
            P(),
            P(),
        ),
        out_specs=P("tm", "space", None, None),
        check_vma=False,
    )
```

```python
import functools

import jax
import jax.numpy as jnp
from jax import lax
from jax.experimental import pallas as pl
from jax.experimental.pallas import tpu as pltpu
from jax.sharding import PartitionSpec as P

EPSILON = 1e-06


def shifted(value, axis, steps):
    count = lax.axis_size(axis)
    leading, last = (max(0, -steps), min(count, count - steps))
    return lax.ppermute(value, axis, [(source, source + steps) for source in range(leading, last)])


def with_halo(block, sides, width):
    for axis, dim in sides:
        count = lax.axis_size(axis)
        forward = [(i, i + 1) for i in range(count - 1)]
        backward = [(target, source) for source, target in forward]
        low = lax.ppermute(
            lax.slice_in_dim(block, block.shape[dim] - width, None, axis=dim), axis, forward
        )
        high = lax.ppermute(lax.slice_in_dim(block, 0, width, axis=dim), axis, backward)
        block = jnp.concatenate([low, block, high], axis=dim)
    return block


def gather_space(block):
    count = lax.axis_size("space")
    rings = count // 4

    def moved(value, target):
        return lax.ppermute(value, "space", [(s, target(s)) for s in range(count)])

    partner = moved(block, lambda s: s ^ 2)
    own = jnp.concatenate([block, partner], axis=0)
    forward = lambda s: ((s // 4 + 1) % rings) * 4 + s % 4
    backward = lambda s: ((s // 4 - 1) % rings) * 4 + s % 4
    batches = [[own]]
    ahead, behind = own, own
    for step in range(rings // 2 - 1):
        ahead = moved(ahead, forward)
        behind = moved(behind, backward)
        batches[-1] += [ahead, behind]
        if step == 0:
            batches.append([])
    half = own.shape[0] // 2
    batches[-1].append(moved(ahead[:half], forward))
    batches[-1].append(moved(behind[half:], backward))
    mine = [jnp.concatenate(batch, axis=0) for batch in batches]
    other = [moved(chunk, lambda s: s ^ 1) for chunk in mine]
    return mine + other


def normalize(frames, norm_gain):
    widened = frames.astype(jnp.float32)
    inverse = lax.rsqrt(jnp.mean(widened * widened, axis=-1, keepdims=True) + EPSILON)
    return (widened * inverse * norm_gain.astype(jnp.float32)).astype(jnp.bfloat16)


def project(rows, weight, bias):
    return (
        jnp.dot(rows, weight, preferred_element_type=jnp.float32) + bias.astype(jnp.float32)
    ).astype(jnp.bfloat16)


def attend(running, queries, key_rows, value_rows):
    best, mass, total_sum = running
    scores = lax.dot_general(
        queries, key_rows, (((1,), (1,)), ((), ())), preferred_element_type=jnp.float32
    ) * queries.shape[1] ** (-0.5)
    new_best = jnp.maximum(best, jnp.max(scores, axis=1, keepdims=True))
    correction = jnp.exp(best - new_best)
    weights = jnp.exp(scores - new_best)
    mass = mass * correction + jnp.sum(weights, axis=1, keepdims=True)
    total_sum = total_sum * correction + jnp.dot(
        weights.astype(jnp.bfloat16), value_rows, preferred_element_type=jnp.float32
    )
    return (new_best, mass, total_sum)

BLOCK = 384


def attention_kernel(*refs, sizes, channels):
    q_ref, gain_ref, wk_ref, bk_ref, wv_ref, bv_ref = refs[:6]
    chunk_refs = refs[6:6 + len(sizes)]
    out_ref = refs[6 + len(sizes)]
    queries = q_ref[...]
    gain = gain_ref[...]
    wk = wk_ref[...]
    wv = wv_ref[...]
    bk = bk_ref[...]
    bv = bv_ref[...]
    count = queries.shape[0]
    best = jnp.full((count, 1), -jnp.inf, jnp.float32)
    mass = jnp.zeros((count, 1), jnp.float32)
    total = jnp.zeros((count, channels), jnp.float32)
    for chunk_ref, size in zip(chunk_refs, sizes):
        for start in range(0, size, BLOCK):
            rows = chunk_ref[start:start + BLOCK, :].astype(jnp.float32)
            inverse = lax.rsqrt(jnp.mean(rows * rows, axis=-1, keepdims=True) + EPSILON)
            normed = (rows * inverse * gain).astype(jnp.bfloat16)
            keys = (jnp.dot(normed, wk, preferred_element_type=jnp.float32) + bk).astype(jnp.bfloat16)
            values = (jnp.dot(normed, wv, preferred_element_type=jnp.float32) + bv).astype(jnp.bfloat16)
            scores = lax.dot_general(
                queries, keys, (((1,), (1,)), ((), ())), preferred_element_type=jnp.float32
            ) * channels ** (-0.5)
            new_best = jnp.maximum(best, jnp.max(scores, axis=1, keepdims=True))
            correction = jnp.exp(best - new_best)
            weights = jnp.exp(scores - new_best)
            mass = mass * correction + jnp.sum(weights, axis=1, keepdims=True)
            total = total * correction + jnp.dot(
                weights.astype(jnp.bfloat16), values, preferred_element_type=jnp.float32
            )
            best = new_best
    out_ref[...] = (total / mass).astype(out_ref.dtype)


def fused_attention(queries, chunks, norm_gain, w_qkv, b_qkv):
    channels = queries.shape[1]
    sizes = tuple(c.shape[0] for c in chunks)
    gain = norm_gain.astype(jnp.float32).reshape(1, channels)
    wk = w_qkv[:, channels:2 * channels]
    wv = w_qkv[:, 2 * channels:]
    bk = b_qkv[channels:2 * channels].astype(jnp.float32).reshape(1, channels)
    bv = b_qkv[2 * channels:].astype(jnp.float32).reshape(1, channels)
    vmem = pltpu.MemorySpace.VMEM
    spec = pl.BlockSpec(memory_space=vmem)
    total_rows = sum(sizes)
    flops = 2 * total_rows * channels * (2 * channels + 2 * queries.shape[0])
    return pl.pallas_call(
        functools.partial(attention_kernel, sizes=sizes, channels=channels),
        out_shape=jax.ShapeDtypeStruct(queries.shape, jnp.bfloat16),
        in_specs=[spec] * (6 + len(chunks)),
        out_specs=spec,
        compiler_params=pltpu.CompilerParams(vmem_limit_bytes=48 * 1024 * 1024),
        cost_estimate=pl.CostEstimate(
            flops=flops,
            transcendentals=total_rows * queries.shape[0],
            bytes_accessed=2 * total_rows * channels + 4 * channels * channels + 4 * queries.size,
        ),
    )(queries, gain, wk, bk, wv, bv, *chunks)


def body(
    frames, cache_in, norm_gain, w_qkv, b_qkv, w_proj, b_proj, w_time, b_time, w_space, b_space
):
    channels = frames.shape[-1]
    rows = frames.shape[1]
    width = frames.shape[2]
    chunks = gather_space(frames.reshape(-1, channels))
    normed = normalize(frames, norm_gain).reshape(-1, channels)
    queries = project(normed, w_qkv[:, :channels], b_qkv[:channels])
    mixed = fused_attention(queries, chunks, norm_gain, w_qkv, b_qkv)
    hidden = (
        frames.reshape(-1, channels).astype(jnp.float32)
        + jnp.dot(mixed, w_proj, preferred_element_type=jnp.float32)
        + b_proj.astype(jnp.float32)
    ).astype(jnp.bfloat16)
    position = lax.axis_index("tm")
    carried = cache_in.reshape(2, -1, channels)
    near_frame = shifted(hidden, "tm", 1)
    near_frame = jnp.where(position == 0, carried[1], near_frame)
    far_frame = shifted(hidden, "tm", 2)
    far_frame = jnp.where(position == 1, carried[1], far_frame)
    far_frame = jnp.where(position == 0, carried[0], far_frame)
    timed = b_time.astype(jnp.float32) + jnp.dot(
        far_frame, w_time[0], preferred_element_type=jnp.float32
    )
    timed = timed + jnp.dot(near_frame, w_time[1], preferred_element_type=jnp.float32)
    timed = (timed + jnp.dot(hidden, w_time[2], preferred_element_type=jnp.float32)).astype(
        jnp.bfloat16
    )
    paired = jnp.stack([timed[:, :channels], timed[:, channels:]]).reshape(2, rows, width, channels)
    padded = with_halo(paired, (("space", 1),), 1)
    upsampled = jnp.repeat(jnp.repeat(padded, 2, axis=1)[:, 1 : 2 * rows + 3], 2, axis=2)
    upsampled = jnp.pad(upsampled, ((0, 0), (0, 0), (1, 1), (0, 0)))
    out_channels = w_space.shape[-1]
    result = jnp.zeros((8 * rows * width, out_channels), jnp.float32) + b_space.astype(jnp.float32)
    for row_tap in range(3):
        for col_tap in range(3):
            window = upsampled[
                :, row_tap : row_tap + 2 * rows, col_tap : col_tap + 2 * width
            ].reshape(-1, channels)
            result = result + jnp.dot(
                window, w_space[row_tap, col_tap], preferred_element_type=jnp.float32
            )
    return result.astype(jnp.bfloat16).reshape(2, 2 * rows, 2 * width, out_channels)


def solution(mesh):
    return jax.shard_map(
        body,
        mesh=mesh,
        in_specs=(
            P("tm", "space", None, None),
            P(None, "space", None, None),
            P(),
            P(),
            P(),
            P(),
            P(),
            P(),
            P(),
            P(),
            P(),
        ),
        out_specs=P("tm", "space", None, None),
        check_vma=False,
    )
```

```python
import functools

import jax
import jax.numpy as jnp
from jax import lax
from jax.experimental import pallas as pl
from jax.experimental.pallas import tpu as pltpu
from jax.sharding import PartitionSpec as P

EPSILON = 1e-06


def shifted(value, axis, steps):
    count = lax.axis_size(axis)
    leading, last = (max(0, -steps), min(count, count - steps))
    return lax.ppermute(value, axis, [(source, source + steps) for source in range(leading, last)])


def with_halo(block, sides, width):
    for axis, dim in sides:
        count = lax.axis_size(axis)
        forward = [(i, i + 1) for i in range(count - 1)]
        backward = [(target, source) for source, target in forward]
        low = lax.ppermute(
            lax.slice_in_dim(block, block.shape[dim] - width, None, axis=dim), axis, forward
        )
        high = lax.ppermute(lax.slice_in_dim(block, 0, width, axis=dim), axis, backward)
        block = jnp.concatenate([low, block, high], axis=dim)
    return block


def gather_space(block):
    count = lax.axis_size("space")
    rings = count // 4

    def moved(value, target):
        return lax.ppermute(value, "space", [(s, target(s)) for s in range(count)])

    partner = moved(block, lambda s: s ^ 2)
    own = jnp.concatenate([block, partner], axis=0)
    forward = lambda s: ((s // 4 + 1) % rings) * 4 + s % 4
    backward = lambda s: ((s // 4 - 1) % rings) * 4 + s % 4
    batches = [[own]]
    ahead, behind = own, own
    for step in range(rings // 2 - 1):
        ahead = moved(ahead, forward)
        behind = moved(behind, backward)
        batches[-1] += [ahead, behind]
        if step == 0:
            batches.append([])
    half = own.shape[0] // 2
    batches[-1].append(moved(ahead[:half], forward))
    batches[-1].append(moved(behind[half:], backward))
    mine = [jnp.concatenate(batch, axis=0) for batch in batches]
    other = [moved(chunk, lambda s: s ^ 1) for chunk in mine]
    return mine + other


def normalize(frames, norm_gain):
    widened = frames.astype(jnp.float32)
    inverse = lax.rsqrt(jnp.mean(widened * widened, axis=-1, keepdims=True) + EPSILON)
    return (widened * inverse * norm_gain.astype(jnp.float32)).astype(jnp.bfloat16)


def project(rows, weight, bias):
    return (
        jnp.dot(rows, weight, preferred_element_type=jnp.float32) + bias.astype(jnp.float32)
    ).astype(jnp.bfloat16)


def attend(running, queries, key_rows, value_rows):
    best, mass, total_sum = running
    scores = lax.dot_general(
        queries, key_rows, (((1,), (1,)), ((), ())), preferred_element_type=jnp.float32
    ) * queries.shape[1] ** (-0.5)
    new_best = jnp.maximum(best, jnp.max(scores, axis=1, keepdims=True))
    correction = jnp.exp(best - new_best)
    weights = jnp.exp(scores - new_best)
    mass = mass * correction + jnp.sum(weights, axis=1, keepdims=True)
    total_sum = total_sum * correction + jnp.dot(
        weights.astype(jnp.bfloat16), value_rows, preferred_element_type=jnp.float32
    )
    return (new_best, mass, total_sum)

BLOCK = 384


def attention_kernel(*refs, sizes, channels):
    q_ref, gain_ref, wk_ref, bk_ref, wv_ref, bv_ref = refs[:6]
    chunk_refs = refs[6:6 + len(sizes)]
    out_ref = refs[6 + len(sizes)]
    queries = q_ref[...]
    gain = gain_ref[...]
    wk = wk_ref[...]
    wv = wv_ref[...]
    bk = bk_ref[...]
    bv = bv_ref[...]
    count = queries.shape[0]
    best = jnp.full((count, 1), -jnp.inf, jnp.float32)
    mass = jnp.zeros((count, 1), jnp.float32)
    total = jnp.zeros((count, channels), jnp.float32)
    for chunk_ref, size in zip(chunk_refs, sizes):
        for start in range(0, size, BLOCK):
            rows = chunk_ref[start:start + BLOCK, :].astype(jnp.float32)
            inverse = lax.rsqrt(jnp.mean(rows * rows, axis=-1, keepdims=True) + EPSILON)
            normed = (rows * inverse * gain).astype(jnp.bfloat16)
            keys = (jnp.dot(normed, wk, preferred_element_type=jnp.float32) + bk).astype(jnp.bfloat16)
            values = (jnp.dot(normed, wv, preferred_element_type=jnp.float32) + bv).astype(jnp.bfloat16)
            scores = lax.dot_general(
                queries, keys, (((1,), (1,)), ((), ())), preferred_element_type=jnp.float32
            ) * channels ** (-0.5)
            new_best = jnp.maximum(best, jnp.max(scores, axis=1, keepdims=True))
            correction = jnp.exp(best - new_best)
            weights = jnp.exp(scores - new_best)
            mass = mass * correction + jnp.sum(weights, axis=1, keepdims=True)
            total = total * correction + jnp.dot(
                weights.astype(jnp.bfloat16), values, preferred_element_type=jnp.float32
            )
            best = new_best
    out_ref[...] = (total / mass).astype(out_ref.dtype)


def fused_attention(queries, chunks, norm_gain, w_qkv, b_qkv):
    channels = queries.shape[1]
    sizes = tuple(c.shape[0] for c in chunks)
    gain = norm_gain.astype(jnp.float32).reshape(1, channels)
    wk = w_qkv[:, channels:2 * channels]
    wv = w_qkv[:, 2 * channels:]
    bk = b_qkv[channels:2 * channels].astype(jnp.float32).reshape(1, channels)
    bv = b_qkv[2 * channels:].astype(jnp.float32).reshape(1, channels)
    vmem = pltpu.MemorySpace.VMEM
    spec = pl.BlockSpec(memory_space=vmem)
    total_rows = sum(sizes)
    flops = 2 * total_rows * channels * (2 * channels + 2 * queries.shape[0])
    return pl.pallas_call(
        functools.partial(attention_kernel, sizes=sizes, channels=channels),
        out_shape=jax.ShapeDtypeStruct(queries.shape, jnp.bfloat16),
        in_specs=[spec] * (6 + len(chunks)),
        out_specs=spec,
        compiler_params=pltpu.CompilerParams(vmem_limit_bytes=48 * 1024 * 1024),
        cost_estimate=pl.CostEstimate(
            flops=flops,
            transcendentals=total_rows * queries.shape[0],
            bytes_accessed=2 * total_rows * channels + 4 * channels * channels + 4 * queries.size,
        ),
    )(queries, gain, wk, bk, wv, bv, *chunks)


def body(
    frames, cache_in, norm_gain, w_qkv, b_qkv, w_proj, b_proj, w_time, b_time, w_space, b_space
):
    channels = frames.shape[-1]
    rows = frames.shape[1]
    width = frames.shape[2]
    chunks = gather_space(frames.reshape(-1, channels))
    normed = normalize(frames, norm_gain).reshape(-1, channels)
    queries = project(normed, w_qkv[:, :channels], b_qkv[:channels])
    mixed = fused_attention(queries, chunks, norm_gain, w_qkv, b_qkv)
    hidden = (
        frames.reshape(-1, channels).astype(jnp.float32)
        + jnp.dot(mixed, w_proj, preferred_element_type=jnp.float32)
        + b_proj.astype(jnp.float32)
    ).astype(jnp.bfloat16)
    position = lax.axis_index("tm")
    carried = cache_in.reshape(2, -1, channels)
    near_frame = shifted(hidden, "tm", 1)
    near_frame = jnp.where(position == 0, carried[1], near_frame)
    far_frame = shifted(hidden, "tm", 2)
    far_frame = jnp.where(position == 1, carried[1], far_frame)
    far_frame = jnp.where(position == 0, carried[0], far_frame)
    timed = b_time.astype(jnp.float32) + jnp.dot(
        far_frame, w_time[0], preferred_element_type=jnp.float32
    )
    timed = timed + jnp.dot(near_frame, w_time[1], preferred_element_type=jnp.float32)
    timed = (timed + jnp.dot(hidden, w_time[2], preferred_element_type=jnp.float32)).astype(
        jnp.bfloat16
    )
    paired = jnp.stack([timed[:, :channels], timed[:, channels:]]).reshape(2, rows, width, channels)
    padded = with_halo(paired, (("space", 1),), 1)
    upsampled = jnp.repeat(padded, 2, axis=1)[:, 1 : 2 * rows + 3]
    upsampled = jnp.pad(upsampled, ((0, 0), (0, 0), (1, 1), (0, 0)))
    out_channels = w_space.shape[-1]
    phases = []
    for offsets in ((0, 1, 1), (1, 1, 2)):
        result = jnp.zeros((4 * rows * width, out_channels), jnp.float32) + b_space.astype(jnp.float32)
        for row_tap in range(3):
            for col_tap in range(3):
                start = offsets[col_tap]
                window = upsampled[
                    :, row_tap : row_tap + 2 * rows, start : start + width
                ].reshape(-1, channels)
                result = result + jnp.dot(
                    window, w_space[row_tap, col_tap], preferred_element_type=jnp.float32
                )
        phases.append(result.astype(jnp.bfloat16).reshape(2, 2 * rows, width, 1, out_channels))
    return jnp.concatenate(phases, axis=3).reshape(2, 2 * rows, 2 * width, out_channels)


def solution(mesh):
    return jax.shard_map(
        body,
        mesh=mesh,
        in_specs=(
            P("tm", "space", None, None),
            P(None, "space", None, None),
            P(),
            P(),
            P(),
            P(),
            P(),
            P(),
            P(),
            P(),
            P(),
        ),
        out_specs=P("tm", "space", None, None),
        check_vma=False,
    )
```

```python
import functools

import jax
import jax.numpy as jnp
from jax import lax
from jax.experimental import pallas as pl
from jax.experimental.pallas import tpu as pltpu
from jax.sharding import PartitionSpec as P

EPSILON = 1e-06


def shifted(value, axis, steps):
    count = lax.axis_size(axis)
    leading, last = (max(0, -steps), min(count, count - steps))
    return lax.ppermute(value, axis, [(source, source + steps) for source in range(leading, last)])


def with_halo(block, sides, width):
    for axis, dim in sides:
        count = lax.axis_size(axis)
        forward = [(i, i + 1) for i in range(count - 1)]
        backward = [(target, source) for source, target in forward]
        low = lax.ppermute(
            lax.slice_in_dim(block, block.shape[dim] - width, None, axis=dim), axis, forward
        )
        high = lax.ppermute(lax.slice_in_dim(block, 0, width, axis=dim), axis, backward)
        block = jnp.concatenate([low, block, high], axis=dim)
    return block


def gather_space(block):
    count = lax.axis_size("space")
    rings = count // 4

    def moved(value, target):
        return lax.ppermute(value, "space", [(s, target(s)) for s in range(count)])

    partner = moved(block, lambda s: s ^ 2)
    own = jnp.concatenate([block, partner], axis=0)
    forward = lambda s: ((s // 4 + 1) % rings) * 4 + s % 4
    backward = lambda s: ((s // 4 - 1) % rings) * 4 + s % 4
    batches = [[own]]
    ahead, behind = own, own
    for step in range(rings // 2 - 1):
        ahead = moved(ahead, forward)
        behind = moved(behind, backward)
        batches[-1] += [ahead, behind]
        if step == 0:
            batches.append([])
    half = own.shape[0] // 2
    batches[-1].append(moved(ahead[:half], forward))
    batches[-1].append(moved(behind[half:], backward))
    mine = [jnp.concatenate(batch, axis=0) for batch in batches]
    other = [moved(chunk, lambda s: s ^ 1) for chunk in mine]
    return mine + other


def normalize(frames, norm_gain):
    widened = frames.astype(jnp.float32)
    inverse = lax.rsqrt(jnp.mean(widened * widened, axis=-1, keepdims=True) + EPSILON)
    return (widened * inverse * norm_gain.astype(jnp.float32)).astype(jnp.bfloat16)


def project(rows, weight, bias):
    return (
        jnp.dot(rows, weight, preferred_element_type=jnp.float32) + bias.astype(jnp.float32)
    ).astype(jnp.bfloat16)


def attend(running, queries, key_rows, value_rows):
    best, mass, total_sum = running
    scores = lax.dot_general(
        queries, key_rows, (((1,), (1,)), ((), ())), preferred_element_type=jnp.float32
    ) * queries.shape[1] ** (-0.5)
    new_best = jnp.maximum(best, jnp.max(scores, axis=1, keepdims=True))
    correction = jnp.exp(best - new_best)
    weights = jnp.exp(scores - new_best)
    mass = mass * correction + jnp.sum(weights, axis=1, keepdims=True)
    total_sum = total_sum * correction + jnp.dot(
        weights.astype(jnp.bfloat16), value_rows, preferred_element_type=jnp.float32
    )
    return (new_best, mass, total_sum)

BLOCK = 384


def attention_kernel(*refs, sizes, channels):
    q_ref, gain_ref, wk_ref, bk_ref, wv_ref, bv_ref = refs[:6]
    chunk_refs = refs[6:6 + len(sizes)]
    out_ref = refs[6 + len(sizes)]
    queries = q_ref[...]
    gain = gain_ref[...]
    wk = wk_ref[...]
    wv = wv_ref[...]
    bk = bk_ref[...]
    bv = bv_ref[...]
    count = queries.shape[0]
    best = jnp.full((count, 1), -jnp.inf, jnp.float32)
    mass = jnp.zeros((count, 1), jnp.float32)
    total = jnp.zeros((count, channels), jnp.float32)
    for chunk_ref, size in zip(chunk_refs, sizes):
        for start in range(0, size, BLOCK):
            rows = chunk_ref[start:start + BLOCK, :].astype(jnp.float32)
            inverse = lax.rsqrt(jnp.mean(rows * rows, axis=-1, keepdims=True) + EPSILON)
            normed = (rows * inverse * gain).astype(jnp.bfloat16)
            keys = (jnp.dot(normed, wk, preferred_element_type=jnp.float32) + bk).astype(jnp.bfloat16)
            values = (jnp.dot(normed, wv, preferred_element_type=jnp.float32) + bv).astype(jnp.bfloat16)
            scores = lax.dot_general(
                queries, keys, (((1,), (1,)), ((), ())), preferred_element_type=jnp.float32
            ) * channels ** (-0.5)
            new_best = jnp.maximum(best, jnp.max(scores, axis=1, keepdims=True))
            correction = jnp.exp(best - new_best)
            weights = jnp.exp(scores - new_best)
            mass = mass * correction + jnp.sum(weights, axis=1, keepdims=True)
            total = total * correction + jnp.dot(
                weights.astype(jnp.bfloat16), values, preferred_element_type=jnp.float32
            )
            best = new_best
    out_ref[...] = (total / mass).astype(out_ref.dtype)


def fused_attention(queries, chunks, norm_gain, w_qkv, b_qkv):
    channels = queries.shape[1]
    sizes = tuple(c.shape[0] for c in chunks)
    gain = norm_gain.astype(jnp.float32).reshape(1, channels)
    wk = w_qkv[:, channels:2 * channels]
    wv = w_qkv[:, 2 * channels:]
    bk = b_qkv[channels:2 * channels].astype(jnp.float32).reshape(1, channels)
    bv = b_qkv[2 * channels:].astype(jnp.float32).reshape(1, channels)
    vmem = pltpu.MemorySpace.VMEM
    spec = pl.BlockSpec(memory_space=vmem)
    total_rows = sum(sizes)
    flops = 2 * total_rows * channels * (2 * channels + 2 * queries.shape[0])
    return pl.pallas_call(
        functools.partial(attention_kernel, sizes=sizes, channels=channels),
        out_shape=jax.ShapeDtypeStruct(queries.shape, jnp.bfloat16),
        in_specs=[spec] * (6 + len(chunks)),
        out_specs=spec,
        compiler_params=pltpu.CompilerParams(vmem_limit_bytes=48 * 1024 * 1024),
        cost_estimate=pl.CostEstimate(
            flops=flops,
            transcendentals=total_rows * queries.shape[0],
            bytes_accessed=2 * total_rows * channels + 4 * channels * channels + 4 * queries.size,
        ),
    )(queries, gain, wk, bk, wv, bv, *chunks)


def body(
    frames, cache_in, norm_gain, w_qkv, b_qkv, w_proj, b_proj, w_time, b_time, w_space, b_space
):
    channels = frames.shape[-1]
    rows = frames.shape[1]
    width = frames.shape[2]
    chunks = gather_space(frames.reshape(-1, channels))
    normed = normalize(frames, norm_gain).reshape(-1, channels)
    queries = project(normed, w_qkv[:, :channels], b_qkv[:channels])
    mixed = fused_attention(queries, chunks, norm_gain, w_qkv, b_qkv)
    hidden = (
        frames.reshape(-1, channels).astype(jnp.float32)
        + jnp.dot(mixed, w_proj, preferred_element_type=jnp.float32)
        + b_proj.astype(jnp.float32)
    ).astype(jnp.bfloat16)
    position = lax.axis_index("tm")
    carried = cache_in.reshape(2, -1, channels)
    near_frame = shifted(hidden, "tm", 1)
    near_frame = jnp.where(position == 0, carried[1], near_frame)
    far_frame = shifted(hidden, "tm", 2)
    far_frame = jnp.where(position == 1, carried[1], far_frame)
    far_frame = jnp.where(position == 0, carried[0], far_frame)
    timed = b_time.astype(jnp.float32) + jnp.dot(
        far_frame, w_time[0], preferred_element_type=jnp.float32
    )
    timed = timed + jnp.dot(near_frame, w_time[1], preferred_element_type=jnp.float32)
    timed = (timed + jnp.dot(hidden, w_time[2], preferred_element_type=jnp.float32)).astype(
        jnp.bfloat16
    )
    paired = jnp.stack([timed[:, :channels], timed[:, channels:]]).reshape(2, rows, width, channels)
    padded = with_halo(paired, (("space", 1),), 1)
    out_channels = w_space.shape[-1]
    row_source = ((0, 1, 1), (1, 1, 2))
    products = {}
    for offset in range(3):
        taps = sorted({row_tap for parity in row_source for row_tap in range(3) if parity[row_tap] == offset})
        lhs = padded[:, offset : offset + rows].reshape(-1, channels)
        rhs = jnp.concatenate([w_space[row_tap, col_tap] for row_tap in taps for col_tap in range(3)], axis=1)
        both = jnp.dot(lhs, rhs, preferred_element_type=jnp.float32)
        both = both.reshape(2, rows, width, len(taps) * 3, out_channels)
        for index, row_tap in enumerate(taps):
            for col_tap in range(3):
                products[offset, row_tap, col_tap] = both[:, :, :, index * 3 + col_tap]

    def shifted_cols(value, steps):
        if steps < 0:
            return jnp.pad(value, ((0, 0), (0, 0), (1, 0), (0, 0)))[:, :, :width]
        return jnp.pad(value, ((0, 0), (0, 0), (0, 1), (0, 0)))[:, :, 1:]

    bias = b_space.astype(jnp.float32)
    rows_out = []
    for parity in row_source:
        taps = [sum(products[parity[row_tap], row_tap, col_tap] for row_tap in range(3)) for col_tap in range(3)]
        even = bias + shifted_cols(taps[0], -1) + taps[1] + taps[2]
        odd = bias + taps[0] + taps[1] + shifted_cols(taps[2], 1)
        rows_out.append(jnp.stack([even, odd], axis=3).astype(jnp.bfloat16))
    result = jnp.stack(rows_out, axis=2)
    return result.reshape(2, 2 * rows, 2 * width, out_channels)


def solution(mesh):
    return jax.shard_map(
        body,
        mesh=mesh,
        in_specs=(
            P("tm", "space", None, None),
            P(None, "space", None, None),
            P(),
            P(),
            P(),
            P(),
            P(),
            P(),
            P(),
            P(),
            P(),
        ),
        out_specs=P("tm", "space", None, None),
        check_vma=False,
    )
```

```python
import functools

import jax
import jax.numpy as jnp
from jax import lax
from jax.experimental import pallas as pl
from jax.experimental.pallas import tpu as pltpu
from jax.sharding import PartitionSpec as P

EPSILON = 1e-06


def shifted(value, axis, steps):
    count = lax.axis_size(axis)
    leading, last = (max(0, -steps), min(count, count - steps))
    return lax.ppermute(value, axis, [(source, source + steps) for source in range(leading, last)])


def with_halo(block, sides, width):
    for axis, dim in sides:
        count = lax.axis_size(axis)
        forward = [(i, i + 1) for i in range(count - 1)]
        backward = [(target, source) for source, target in forward]
        low = lax.ppermute(
            lax.slice_in_dim(block, block.shape[dim] - width, None, axis=dim), axis, forward
        )
        high = lax.ppermute(lax.slice_in_dim(block, 0, width, axis=dim), axis, backward)
        block = jnp.concatenate([low, block, high], axis=dim)
    return block


def gather_space(block):
    count = lax.axis_size("space")
    rings = count // 4

    def moved(value, target):
        return lax.ppermute(value, "space", [(s, target(s)) for s in range(count)])

    partner = moved(block, lambda s: s ^ 2)
    own = jnp.concatenate([block, partner], axis=0)
    forward = lambda s: ((s // 4 + 1) % rings) * 4 + s % 4
    backward = lambda s: ((s // 4 - 1) % rings) * 4 + s % 4
    batches = [[own]]
    ahead, behind = own, own
    for step in range(rings // 2 - 1):
        ahead = moved(ahead, forward)
        behind = moved(behind, backward)
        batches[-1] += [ahead, behind]
        if step == 0:
            batches.append([])
    half = own.shape[0] // 2
    batches[-1].append(moved(ahead[:half], forward))
    batches[-1].append(moved(behind[half:], backward))
    mine = [jnp.concatenate(batch, axis=0) for batch in batches]
    other = [moved(chunk, lambda s: s ^ 1) for chunk in mine]
    return mine + other


def normalize(frames, norm_gain):
    widened = frames.astype(jnp.float32)
    inverse = lax.rsqrt(jnp.mean(widened * widened, axis=-1, keepdims=True) + EPSILON)
    return (widened * inverse * norm_gain.astype(jnp.float32)).astype(jnp.bfloat16)


def project(rows, weight, bias):
    return (
        jnp.dot(rows, weight, preferred_element_type=jnp.float32) + bias.astype(jnp.float32)
    ).astype(jnp.bfloat16)


def attend(running, queries, key_rows, value_rows):
    best, mass, total_sum = running
    scores = lax.dot_general(
        queries, key_rows, (((1,), (1,)), ((), ())), preferred_element_type=jnp.float32
    ) * queries.shape[1] ** (-0.5)
    new_best = jnp.maximum(best, jnp.max(scores, axis=1, keepdims=True))
    correction = jnp.exp(best - new_best)
    weights = jnp.exp(scores - new_best)
    mass = mass * correction + jnp.sum(weights, axis=1, keepdims=True)
    total_sum = total_sum * correction + jnp.dot(
        weights.astype(jnp.bfloat16), value_rows, preferred_element_type=jnp.float32
    )
    return (new_best, mass, total_sum)

BLOCK = 384


def attention_kernel(*refs, sizes, channels, resume, finish):
    q_ref, gain_ref, wk_ref, bk_ref, wv_ref, bv_ref = refs[:6]
    chunk_refs = refs[6:6 + len(sizes)]
    rest = refs[6 + len(sizes):]
    queries = q_ref[...]
    gain = gain_ref[...]
    wk = wk_ref[...]
    wv = wv_ref[...]
    bk = bk_ref[...]
    bv = bv_ref[...]
    count = queries.shape[0]
    if resume:
        best, mass, total = rest[0][...], rest[1][...], rest[2][...]
        rest = rest[3:]
    else:
        best = jnp.full((count, 1), -jnp.inf, jnp.float32)
        mass = jnp.zeros((count, 1), jnp.float32)
        total = jnp.zeros((count, channels), jnp.float32)
    for chunk_ref, size in zip(chunk_refs, sizes):
        for start in range(0, size, BLOCK):
            rows = chunk_ref[start:start + BLOCK, :].astype(jnp.float32)
            inverse = lax.rsqrt(jnp.mean(rows * rows, axis=-1, keepdims=True) + EPSILON)
            normed = (rows * inverse * gain).astype(jnp.bfloat16)
            keys = (jnp.dot(normed, wk, preferred_element_type=jnp.float32) + bk).astype(jnp.bfloat16)
            values = (jnp.dot(normed, wv, preferred_element_type=jnp.float32) + bv).astype(jnp.bfloat16)
            scores = lax.dot_general(
                queries, keys, (((1,), (1,)), ((), ())), preferred_element_type=jnp.float32
            ) * channels ** (-0.5)
            new_best = jnp.maximum(best, jnp.max(scores, axis=1, keepdims=True))
            correction = jnp.exp(best - new_best)
            weights = jnp.exp(scores - new_best)
            mass = mass * correction + jnp.sum(weights, axis=1, keepdims=True)
            total = total * correction + jnp.dot(
                weights.astype(jnp.bfloat16), values, preferred_element_type=jnp.float32
            )
            best = new_best
    if finish:
        rest[0][...] = (total / mass).astype(rest[0].dtype)
    else:
        rest[0][...] = best
        rest[1][...] = mass
        rest[2][...] = total


def fused_attention(queries, chunks, norm_gain, w_qkv, b_qkv, state=None, finish=True):
    channels = queries.shape[1]
    count = queries.shape[0]
    sizes = tuple(c.shape[0] for c in chunks)
    gain = norm_gain.astype(jnp.float32).reshape(1, channels)
    wk = w_qkv[:, channels:2 * channels]
    wv = w_qkv[:, 2 * channels:]
    bk = b_qkv[channels:2 * channels].astype(jnp.float32).reshape(1, channels)
    bv = b_qkv[2 * channels:].astype(jnp.float32).reshape(1, channels)
    spec = pl.BlockSpec(memory_space=pltpu.MemorySpace.VMEM)
    total_rows = sum(sizes)
    flops = 2 * total_rows * channels * (2 * channels + 2 * count)
    extra = tuple(state) if state is not None else ()
    if finish:
        out_shape = jax.ShapeDtypeStruct(queries.shape, jnp.bfloat16)
        out_specs = spec
    else:
        out_shape = (
            jax.ShapeDtypeStruct((count, 1), jnp.float32),
            jax.ShapeDtypeStruct((count, 1), jnp.float32),
            jax.ShapeDtypeStruct((count, channels), jnp.float32),
        )
        out_specs = (spec, spec, spec)
    return pl.pallas_call(
        functools.partial(
            attention_kernel, sizes=sizes, channels=channels, resume=state is not None, finish=finish
        ),
        out_shape=out_shape,
        in_specs=[spec] * (6 + len(chunks) + len(extra)),
        out_specs=out_specs,
        compiler_params=pltpu.CompilerParams(vmem_limit_bytes=48 * 1024 * 1024),
        cost_estimate=pl.CostEstimate(
            flops=flops,
            transcendentals=total_rows * count,
            bytes_accessed=2 * total_rows * channels + 4 * channels * channels + 4 * queries.size,
        ),
    )(queries, gain, wk, bk, wv, bv, *chunks, *extra)


def body(
    frames, cache_in, norm_gain, w_qkv, b_qkv, w_proj, b_proj, w_time, b_time, w_space, b_space
):
    channels = frames.shape[-1]
    rows = frames.shape[1]
    width = frames.shape[2]
    chunks = gather_space(frames.reshape(-1, channels))
    normed = normalize(frames, norm_gain).reshape(-1, channels)
    queries = project(normed, w_qkv[:, :channels], b_qkv[:channels])
    half = len(chunks) // 2
    state = fused_attention(queries, chunks[:half], norm_gain, w_qkv, b_qkv, finish=False)
    mixed = fused_attention(queries, chunks[half:], norm_gain, w_qkv, b_qkv, state=state)
    hidden = (
        frames.reshape(-1, channels).astype(jnp.float32)
        + jnp.dot(mixed, w_proj, preferred_element_type=jnp.float32)
        + b_proj.astype(jnp.float32)
    ).astype(jnp.bfloat16)
    position = lax.axis_index("tm")
    carried = cache_in.reshape(2, -1, channels)
    near_frame = shifted(hidden, "tm", 1)
    near_frame = jnp.where(position == 0, carried[1], near_frame)
    far_frame = shifted(hidden, "tm", 2)
    far_frame = jnp.where(position == 1, carried[1], far_frame)
    far_frame = jnp.where(position == 0, carried[0], far_frame)
    timed = b_time.astype(jnp.float32) + jnp.dot(
        far_frame, w_time[0], preferred_element_type=jnp.float32
    )
    timed = timed + jnp.dot(near_frame, w_time[1], preferred_element_type=jnp.float32)
    timed = (timed + jnp.dot(hidden, w_time[2], preferred_element_type=jnp.float32)).astype(
        jnp.bfloat16
    )
    paired = jnp.stack([timed[:, :channels], timed[:, channels:]]).reshape(2, rows, width, channels)
    padded = with_halo(paired, (("space", 1),), 1)
    out_channels = w_space.shape[-1]
    row_source = ((0, 1, 1), (1, 1, 2))
    products = {}
    for offset in range(3):
        taps = sorted({row_tap for parity in row_source for row_tap in range(3) if parity[row_tap] == offset})
        lhs = padded[:, offset : offset + rows].reshape(-1, channels)
        rhs = jnp.concatenate([w_space[row_tap, col_tap] for row_tap in taps for col_tap in range(3)], axis=1)
        both = jnp.dot(lhs, rhs, preferred_element_type=jnp.float32)
        both = both.reshape(2, rows, width, len(taps) * 3, out_channels)
        for index, row_tap in enumerate(taps):
            for col_tap in range(3):
                products[offset, row_tap, col_tap] = both[:, :, :, index * 3 + col_tap]

    def shifted_cols(value, steps):
        if steps < 0:
            return jnp.pad(value, ((0, 0), (0, 0), (1, 0), (0, 0)))[:, :, :width]
        return jnp.pad(value, ((0, 0), (0, 0), (0, 1), (0, 0)))[:, :, 1:]

    bias = b_space.astype(jnp.float32)
    rows_out = []
    for parity in row_source:
        taps = [sum(products[parity[row_tap], row_tap, col_tap] for row_tap in range(3)) for col_tap in range(3)]
        even = bias + shifted_cols(taps[0], -1) + taps[1] + taps[2]
        odd = bias + taps[0] + taps[1] + shifted_cols(taps[2], 1)
        rows_out.append(jnp.stack([even, odd], axis=3).astype(jnp.bfloat16))
    result = jnp.stack(rows_out, axis=2)
    return result.reshape(2, 2 * rows, 2 * width, out_channels)


def solution(mesh):
    return jax.shard_map(
        body,
        mesh=mesh,
        in_specs=(
            P("tm", "space", None, None),
            P(None, "space", None, None),
            P(),
            P(),
            P(),
            P(),
            P(),
            P(),
            P(),
            P(),
            P(),
        ),
        out_specs=P("tm", "space", None, None),
        check_vma=False,
    )
```

```python
import functools

import jax
import jax.numpy as jnp
from jax import lax
from jax.experimental import pallas as pl
from jax.experimental.pallas import tpu as pltpu
from jax.sharding import PartitionSpec as P

EPSILON = 1e-06


def shifted(value, axis, steps):
    count = lax.axis_size(axis)
    leading, last = (max(0, -steps), min(count, count - steps))
    return lax.ppermute(value, axis, [(source, source + steps) for source in range(leading, last)])


def with_halo(block, sides, width):
    for axis, dim in sides:
        count = lax.axis_size(axis)
        forward = [(i, i + 1) for i in range(count - 1)]
        backward = [(target, source) for source, target in forward]
        low = lax.ppermute(
            lax.slice_in_dim(block, block.shape[dim] - width, None, axis=dim), axis, forward
        )
        high = lax.ppermute(lax.slice_in_dim(block, 0, width, axis=dim), axis, backward)
        block = jnp.concatenate([low, block, high], axis=dim)
    return block


def gather_space(block, riders):
    count = lax.axis_size("space")
    rings = count // 4

    def moved(value, target):
        return lax.ppermute(value, "space", [(s, target(s)) for s in range(count)])

    partner = moved(block, lambda s: s ^ 2)
    own = jnp.concatenate([block, partner], axis=0)
    forward = lambda s: ((s // 4 + 1) % rings) * 4 + s % 4
    backward = lambda s: ((s // 4 - 1) % rings) * 4 + s % 4
    batches = [[own]]
    ahead, behind = own, own
    for step in range(rings // 2 - 1):
        ahead = moved(ahead, forward)
        behind = moved(behind, backward)
        if step == 0:
            ahead, behind, riders = lax.optimization_barrier((ahead, behind, riders))
        batches[-1] += [ahead, behind]
        if step == 0:
            batches.append([])
    half = own.shape[0] // 2
    batches[-1].append(moved(ahead[:half], forward))
    batches[-1].append(moved(behind[half:], backward))
    mine = [jnp.concatenate(batch, axis=0) for batch in batches]
    other = [moved(chunk, lambda s: s ^ 1) for chunk in mine]
    return mine + other, riders


def normalize(frames, norm_gain):
    widened = frames.astype(jnp.float32)
    inverse = lax.rsqrt(jnp.mean(widened * widened, axis=-1, keepdims=True) + EPSILON)
    return (widened * inverse * norm_gain.astype(jnp.float32)).astype(jnp.bfloat16)


def project(rows, weight, bias):
    return (
        jnp.dot(rows, weight, preferred_element_type=jnp.float32) + bias.astype(jnp.float32)
    ).astype(jnp.bfloat16)


def attend(running, queries, key_rows, value_rows):
    best, mass, total_sum = running
    scores = lax.dot_general(
        queries, key_rows, (((1,), (1,)), ((), ())), preferred_element_type=jnp.float32
    ) * queries.shape[1] ** (-0.5)
    new_best = jnp.maximum(best, jnp.max(scores, axis=1, keepdims=True))
    correction = jnp.exp(best - new_best)
    weights = jnp.exp(scores - new_best)
    mass = mass * correction + jnp.sum(weights, axis=1, keepdims=True)
    total_sum = total_sum * correction + jnp.dot(
        weights.astype(jnp.bfloat16), value_rows, preferred_element_type=jnp.float32
    )
    return (new_best, mass, total_sum)

BLOCK = 768


def attention_kernel(*refs, sizes, channels, resume, finish):
    q_ref, gain_ref, wkv_ref, bkv_ref = refs[:4]
    chunk_refs = refs[4:4 + len(sizes)]
    rest = refs[4 + len(sizes):]
    queries = q_ref[...]
    gain = gain_ref[...]
    wkv = wkv_ref[...]
    bkv = bkv_ref[...]
    count = queries.shape[0]
    if resume:
        best, mass, total = rest[0][...], rest[1][...], rest[2][...]
        rest = rest[3:]
    else:
        best = jnp.full((count, 1), -jnp.inf, jnp.float32)
        mass = jnp.zeros((count, 1), jnp.float32)
        total = jnp.zeros((count, channels), jnp.float32)
    for chunk_ref, size in zip(chunk_refs, sizes):
        for start in range(0, size, BLOCK):
            rows = chunk_ref[start:min(start + BLOCK, size), :].astype(jnp.float32)
            inverse = lax.rsqrt(jnp.mean(rows * rows, axis=-1, keepdims=True) + EPSILON)
            normed = (rows * inverse * gain).astype(jnp.bfloat16)
            both = (jnp.dot(normed, wkv, preferred_element_type=jnp.float32) + bkv).astype(jnp.bfloat16)
            keys = both[:, :channels]
            values = both[:, channels:]
            scores = lax.dot_general(
                queries, keys, (((1,), (1,)), ((), ())), preferred_element_type=jnp.float32
            ) * channels ** (-0.5)
            new_best = jnp.maximum(best, jnp.max(scores, axis=1, keepdims=True))
            correction = jnp.exp(best - new_best)
            weights = jnp.exp(scores - new_best)
            mass = mass * correction + jnp.sum(weights, axis=1, keepdims=True)
            total = total * correction + jnp.dot(
                weights.astype(jnp.bfloat16), values, preferred_element_type=jnp.float32
            )
            best = new_best
    if finish:
        rest[0][...] = (total / mass).astype(rest[0].dtype)
    else:
        rest[0][...] = best
        rest[1][...] = mass
        rest[2][...] = total


def attention_weights(norm_gain, w_qkv, b_qkv):
    channels = w_qkv.shape[0]
    gain = norm_gain.astype(jnp.float32).reshape(1, channels)
    wkv = w_qkv[:, channels:]
    bkv = b_qkv[channels:].astype(jnp.float32).reshape(1, 2 * channels)
    return gain, wkv, bkv


def fused_attention(queries, chunks, weights, state=None, finish=True):
    channels = queries.shape[1]
    count = queries.shape[0]
    sizes = tuple(c.shape[0] for c in chunks)
    gain, wkv, bkv = weights
    spec = pl.BlockSpec(memory_space=pltpu.MemorySpace.VMEM)
    total_rows = sum(sizes)
    flops = 2 * total_rows * channels * (2 * channels + 2 * count)
    extra = tuple(state) if state is not None else ()
    if finish:
        out_shape = jax.ShapeDtypeStruct(queries.shape, jnp.bfloat16)
        out_specs = spec
    else:
        out_shape = (
            jax.ShapeDtypeStruct((count, 1), jnp.float32),
            jax.ShapeDtypeStruct((count, 1), jnp.float32),
            jax.ShapeDtypeStruct((count, channels), jnp.float32),
        )
        out_specs = (spec, spec, spec)
    return pl.pallas_call(
        functools.partial(
            attention_kernel, sizes=sizes, channels=channels, resume=state is not None, finish=finish
        ),
        out_shape=out_shape,
        in_specs=[spec] * (4 + len(chunks) + len(extra)),
        out_specs=out_specs,
        compiler_params=pltpu.CompilerParams(vmem_limit_bytes=48 * 1024 * 1024),
        cost_estimate=pl.CostEstimate(
            flops=flops,
            transcendentals=total_rows * count,
            bytes_accessed=2 * total_rows * channels + 4 * channels * channels + 4 * queries.size,
        ),
    )(queries, gain, wkv, bkv, *chunks, *extra)


def body(
    frames, cache_in, norm_gain, w_qkv, b_qkv, w_proj, b_proj, w_time, b_time, w_space, b_space
):
    channels = frames.shape[-1]
    rows = frames.shape[1]
    width = frames.shape[2]
    out_channels = w_space.shape[-1]
    row_source = ((0, 1, 1), (1, 1, 2))
    tap_lists = [
        sorted({row_tap for parity in row_source for row_tap in range(3) if parity[row_tap] == offset})
        for offset in range(3)
    ]
    normed = normalize(frames, norm_gain).reshape(-1, channels)
    riders = dict(
        queries=project(normed, w_qkv[:, :channels], b_qkv[:channels]),
        weights=attention_weights(norm_gain, w_qkv, b_qkv),
        conv=[
            jnp.concatenate([w_space[row_tap, col_tap] for row_tap in taps for col_tap in range(3)], axis=1)
            for taps in tap_lists
        ],
        b_proj=b_proj.astype(jnp.float32),
        b_time=b_time.astype(jnp.float32),
        b_space=b_space.astype(jnp.float32),
    )
    chunks, riders = gather_space(frames.reshape(-1, channels), riders)
    queries = riders["queries"]
    half = len(chunks) // 2
    state = fused_attention(queries, chunks[:half], riders["weights"], finish=False)
    mixed = fused_attention(queries, chunks[half:], riders["weights"], state=state)
    hidden = (
        frames.reshape(-1, channels).astype(jnp.float32)
        + jnp.dot(mixed, w_proj, preferred_element_type=jnp.float32)
        + riders["b_proj"]
    ).astype(jnp.bfloat16)
    position = lax.axis_index("tm")
    carried = cache_in.reshape(2, -1, channels)
    near_frame = shifted(hidden, "tm", 1)
    near_frame = jnp.where(position == 0, carried[1], near_frame)
    far_frame = shifted(hidden, "tm", 2)
    far_frame = jnp.where(position == 1, carried[1], far_frame)
    far_frame = jnp.where(position == 0, carried[0], far_frame)
    timed = riders["b_time"] + jnp.dot(
        far_frame, w_time[0], preferred_element_type=jnp.float32
    )
    timed = timed + jnp.dot(near_frame, w_time[1], preferred_element_type=jnp.float32)
    timed = (timed + jnp.dot(hidden, w_time[2], preferred_element_type=jnp.float32)).astype(
        jnp.bfloat16
    )
    paired = jnp.stack([timed[:, :channels], timed[:, channels:]]).reshape(2, rows, width, channels)
    padded = with_halo(paired, (("space", 1),), 1)
    products = {}
    for offset in range(3):
        taps = tap_lists[offset]
        lhs = padded[:, offset : offset + rows].reshape(-1, channels)
        both = jnp.dot(lhs, riders["conv"][offset], preferred_element_type=jnp.float32)
        both = both.reshape(2, rows, width, len(taps) * 3, out_channels)
        for index, row_tap in enumerate(taps):
            for col_tap in range(3):
                products[offset, row_tap, col_tap] = both[:, :, :, index * 3 + col_tap]

    def shifted_cols(value, steps):
        if steps < 0:
            return jnp.pad(value, ((0, 0), (0, 0), (1, 0), (0, 0)))[:, :, :width]
        return jnp.pad(value, ((0, 0), (0, 0), (0, 1), (0, 0)))[:, :, 1:]

    bias = riders["b_space"]
    rows_out = []
    for parity in row_source:
        taps = [sum(products[parity[row_tap], row_tap, col_tap] for row_tap in range(3)) for col_tap in range(3)]
        even = bias + shifted_cols(taps[0], -1) + taps[1] + taps[2]
        odd = bias + taps[0] + taps[1] + shifted_cols(taps[2], 1)
        rows_out.append(jnp.stack([even, odd], axis=3).astype(jnp.bfloat16))
    result = jnp.stack(rows_out, axis=2)
    return result.reshape(2, 2 * rows, 2 * width, out_channels)


def solution(mesh):
    return jax.shard_map(
        body,
        mesh=mesh,
        in_specs=(
            P("tm", "space", None, None),
            P(None, "space", None, None),
            P(),
            P(),
            P(),
            P(),
            P(),
            P(),
            P(),
            P(),
            P(),
        ),
        out_specs=P("tm", "space", None, None),
        check_vma=False,
    )
```

```python
import functools

import jax
import jax.numpy as jnp
from jax import lax
from jax.experimental import pallas as pl
from jax.experimental.pallas import tpu as pltpu
from jax.sharding import PartitionSpec as P

EPSILON = 1e-06


def shifted(value, axis, steps):
    count = lax.axis_size(axis)
    leading, last = (max(0, -steps), min(count, count - steps))
    return lax.ppermute(value, axis, [(source, source + steps) for source in range(leading, last)])


def with_halo(block, sides, width):
    for axis, dim in sides:
        count = lax.axis_size(axis)
        forward = [(i, i + 1) for i in range(count - 1)]
        backward = [(target, source) for source, target in forward]
        low = lax.ppermute(
            lax.slice_in_dim(block, block.shape[dim] - width, None, axis=dim), axis, forward
        )
        high = lax.ppermute(lax.slice_in_dim(block, 0, width, axis=dim), axis, backward)
        block = jnp.concatenate([low, block, high], axis=dim)
    return block


def gather_space(block, riders):
    count = lax.axis_size("space")
    rings = count // 4

    def moved(value, target):
        return lax.ppermute(value, "space", [(s, target(s)) for s in range(count)])

    partner = moved(block, lambda s: s ^ 2)
    own = jnp.concatenate([block, partner], axis=0)
    forward = lambda s: ((s // 4 + 1) % rings) * 4 + s % 4
    backward = lambda s: ((s // 4 - 1) % rings) * 4 + s % 4
    batches = [[own]]
    ahead, behind = own, own
    for step in range(rings // 2 - 1):
        ahead = moved(ahead, forward)
        behind = moved(behind, backward)
        if step == 0:
            ahead, behind, riders = lax.optimization_barrier((ahead, behind, riders))
        if step == 1:
            ahead, behind, early = lax.optimization_barrier((ahead, behind, early))
        batches[-1] += [ahead, behind]
        if step == 0:
            early = moved(jnp.concatenate(batches[0], axis=0), lambda s: s ^ 1)
            batches.append([])
    half = own.shape[0] // 2
    batches[-1].append(moved(ahead[:half], forward))
    batches[-1].append(moved(behind[half:], backward))
    mine = [jnp.concatenate(batch, axis=0) for batch in batches]
    return mine + [early, moved(mine[1], lambda s: s ^ 1)], riders


def normalize(frames, norm_gain):
    widened = frames.astype(jnp.float32)
    inverse = lax.rsqrt(jnp.mean(widened * widened, axis=-1, keepdims=True) + EPSILON)
    return (widened * inverse * norm_gain.astype(jnp.float32)).astype(jnp.bfloat16)


def project(rows, weight, bias):
    return (
        jnp.dot(rows, weight, preferred_element_type=jnp.float32) + bias.astype(jnp.float32)
    ).astype(jnp.bfloat16)


def attend(running, queries, key_rows, value_rows):
    best, mass, total_sum = running
    scores = lax.dot_general(
        queries, key_rows, (((1,), (1,)), ((), ())), preferred_element_type=jnp.float32
    ) * queries.shape[1] ** (-0.5)
    new_best = jnp.maximum(best, jnp.max(scores, axis=1, keepdims=True))
    correction = jnp.exp(best - new_best)
    weights = jnp.exp(scores - new_best)
    mass = mass * correction + jnp.sum(weights, axis=1, keepdims=True)
    total_sum = total_sum * correction + jnp.dot(
        weights.astype(jnp.bfloat16), value_rows, preferred_element_type=jnp.float32
    )
    return (new_best, mass, total_sum)

BLOCK = 768


def attention_kernel(*refs, sizes, channels, resume, finish):
    q_ref, gain_ref, wkv_ref, bkv_ref = refs[:4]
    chunk_refs = refs[4:4 + len(sizes)]
    rest = refs[4 + len(sizes):]
    queries = q_ref[...]
    gain = gain_ref[...]
    wkv = wkv_ref[...]
    bkv = bkv_ref[...]
    count = queries.shape[0]
    if resume:
        best, mass, total = rest[0][...], rest[1][...], rest[2][...]
        rest = rest[3:]
    else:
        best = jnp.full((count, 1), -jnp.inf, jnp.float32)
        mass = jnp.zeros((count, 1), jnp.float32)
        total = jnp.zeros((count, channels), jnp.float32)
    for chunk_ref, size in zip(chunk_refs, sizes):
        for start in range(0, size, BLOCK):
            rows = chunk_ref[start:min(start + BLOCK, size), :].astype(jnp.float32)
            inverse = lax.rsqrt(jnp.mean(rows * rows, axis=-1, keepdims=True) + EPSILON)
            normed = (rows * inverse * gain).astype(jnp.bfloat16)
            both = (jnp.dot(normed, wkv, preferred_element_type=jnp.float32) + bkv).astype(jnp.bfloat16)
            keys = both[:, :channels]
            values = both[:, channels:]
            scores = lax.dot_general(
                queries, keys, (((1,), (1,)), ((), ())), preferred_element_type=jnp.float32
            ) * channels ** (-0.5)
            new_best = jnp.maximum(best, jnp.max(scores, axis=1, keepdims=True))
            correction = jnp.exp(best - new_best)
            weights = jnp.exp(scores - new_best)
            mass = mass * correction + jnp.sum(weights, axis=1, keepdims=True)
            total = total * correction + jnp.dot(
                weights.astype(jnp.bfloat16), values, preferred_element_type=jnp.float32
            )
            best = new_best
    if finish:
        rest[0][...] = (total / mass).astype(rest[0].dtype)
    else:
        rest[0][...] = best
        rest[1][...] = mass
        rest[2][...] = total


def attention_weights(norm_gain, w_qkv, b_qkv):
    channels = w_qkv.shape[0]
    gain = norm_gain.astype(jnp.float32).reshape(1, channels)
    wkv = w_qkv[:, channels:]
    bkv = b_qkv[channels:].astype(jnp.float32).reshape(1, 2 * channels)
    return gain, wkv, bkv


def fused_attention(queries, chunks, weights, state=None, finish=True):
    channels = queries.shape[1]
    count = queries.shape[0]
    sizes = tuple(c.shape[0] for c in chunks)
    gain, wkv, bkv = weights
    spec = pl.BlockSpec(memory_space=pltpu.MemorySpace.VMEM)
    total_rows = sum(sizes)
    flops = 2 * total_rows * channels * (2 * channels + 2 * count)
    extra = tuple(state) if state is not None else ()
    if finish:
        out_shape = jax.ShapeDtypeStruct(queries.shape, jnp.bfloat16)
        out_specs = spec
    else:
        out_shape = (
            jax.ShapeDtypeStruct((count, 1), jnp.float32),
            jax.ShapeDtypeStruct((count, 1), jnp.float32),
            jax.ShapeDtypeStruct((count, channels), jnp.float32),
        )
        out_specs = (spec, spec, spec)
    return pl.pallas_call(
        functools.partial(
            attention_kernel, sizes=sizes, channels=channels, resume=state is not None, finish=finish
        ),
        out_shape=out_shape,
        in_specs=[spec] * (4 + len(chunks) + len(extra)),
        out_specs=out_specs,
        compiler_params=pltpu.CompilerParams(vmem_limit_bytes=48 * 1024 * 1024),
        cost_estimate=pl.CostEstimate(
            flops=flops,
            transcendentals=total_rows * count,
            bytes_accessed=2 * total_rows * channels + 4 * channels * channels + 4 * queries.size,
        ),
    )(queries, gain, wkv, bkv, *chunks, *extra)


def body(
    frames, cache_in, norm_gain, w_qkv, b_qkv, w_proj, b_proj, w_time, b_time, w_space, b_space
):
    channels = frames.shape[-1]
    rows = frames.shape[1]
    width = frames.shape[2]
    out_channels = w_space.shape[-1]
    row_source = ((0, 1, 1), (1, 1, 2))
    tap_lists = [
        sorted({row_tap for parity in row_source for row_tap in range(3) if parity[row_tap] == offset})
        for offset in range(3)
    ]
    normed = normalize(frames, norm_gain).reshape(-1, channels)
    riders = dict(
        queries=project(normed, w_qkv[:, :channels], b_qkv[:channels]),
        weights=attention_weights(norm_gain, w_qkv, b_qkv),
        conv=[
            jnp.concatenate([w_space[row_tap, col_tap] for row_tap in taps for col_tap in range(3)], axis=1)
            for taps in tap_lists
        ],
        b_proj=b_proj.astype(jnp.float32),
        b_time=b_time.astype(jnp.float32),
        b_space=b_space.astype(jnp.float32),
    )
    chunks, riders = gather_space(frames.reshape(-1, channels), riders)
    queries = riders["queries"]
    state = fused_attention(queries, chunks[:-1], riders["weights"], finish=False)
    mixed = fused_attention(queries, chunks[-1:], riders["weights"], state=state)
    hidden = (
        frames.reshape(-1, channels).astype(jnp.float32)
        + jnp.dot(mixed, w_proj, preferred_element_type=jnp.float32)
        + riders["b_proj"]
    ).astype(jnp.bfloat16)
    position = lax.axis_index("tm")
    carried = cache_in.reshape(2, -1, channels)
    near_frame = shifted(hidden, "tm", 1)
    near_frame = jnp.where(position == 0, carried[1], near_frame)
    far_frame = shifted(hidden, "tm", 2)
    far_frame = jnp.where(position == 1, carried[1], far_frame)
    far_frame = jnp.where(position == 0, carried[0], far_frame)
    timed = riders["b_time"] + jnp.dot(
        far_frame, w_time[0], preferred_element_type=jnp.float32
    )
    timed = timed + jnp.dot(near_frame, w_time[1], preferred_element_type=jnp.float32)
    timed = (timed + jnp.dot(hidden, w_time[2], preferred_element_type=jnp.float32)).astype(
        jnp.bfloat16
    )
    paired = jnp.stack([timed[:, :channels], timed[:, channels:]]).reshape(2, rows, width, channels)
    padded = with_halo(paired, (("space", 1),), 1)
    products = {}
    for offset in range(3):
        taps = tap_lists[offset]
        lhs = padded[:, offset : offset + rows].reshape(-1, channels)
        both = jnp.dot(lhs, riders["conv"][offset], preferred_element_type=jnp.float32)
        both = both.reshape(2, rows, width, len(taps) * 3, out_channels)
        for index, row_tap in enumerate(taps):
            for col_tap in range(3):
                products[offset, row_tap, col_tap] = both[:, :, :, index * 3 + col_tap]

    def shifted_cols(value, steps):
        if steps < 0:
            return jnp.pad(value, ((0, 0), (0, 0), (1, 0), (0, 0)))[:, :, :width]
        return jnp.pad(value, ((0, 0), (0, 0), (0, 1), (0, 0)))[:, :, 1:]

    bias = riders["b_space"]
    rows_out = []
    for parity in row_source:
        taps = [sum(products[parity[row_tap], row_tap, col_tap] for row_tap in range(3)) for col_tap in range(3)]
        even = bias + shifted_cols(taps[0], -1) + taps[1] + taps[2]
        odd = bias + taps[0] + taps[1] + shifted_cols(taps[2], 1)
        rows_out.append(jnp.stack([even, odd], axis=3).astype(jnp.bfloat16))
    result = jnp.stack(rows_out, axis=2)
    return result.reshape(2, 2 * rows, 2 * width, out_channels)


def solution(mesh):
    return jax.shard_map(
        body,
        mesh=mesh,
        in_specs=(
            P("tm", "space", None, None),
            P(None, "space", None, None),
            P(),
            P(),
            P(),
            P(),
            P(),
            P(),
            P(),
            P(),
            P(),
        ),
        out_specs=P("tm", "space", None, None),
        check_vma=False,
    )
```

```python
import functools

import jax
import jax.numpy as jnp
from jax import lax
from jax.experimental import pallas as pl
from jax.experimental.pallas import tpu as pltpu
from jax.sharding import PartitionSpec as P

EPSILON = 1e-06


def shifted(value, axis, steps):
    count = lax.axis_size(axis)
    leading, last = (max(0, -steps), min(count, count - steps))
    return lax.ppermute(value, axis, [(source, source + steps) for source in range(leading, last)])


def with_halo(block, sides, width):
    for axis, dim in sides:
        count = lax.axis_size(axis)
        forward = [(i, i + 1) for i in range(count - 1)]
        backward = [(target, source) for source, target in forward]
        low = lax.ppermute(
            lax.slice_in_dim(block, block.shape[dim] - width, None, axis=dim), axis, forward
        )
        high = lax.ppermute(lax.slice_in_dim(block, 0, width, axis=dim), axis, backward)
        block = jnp.concatenate([low, block, high], axis=dim)
    return block


def gather_space(block, riders):
    count = lax.axis_size("space")
    rings = count // 4

    def moved(value, target):
        return lax.ppermute(value, "space", [(s, target(s)) for s in range(count)])

    partner = moved(block, lambda s: s ^ 2)
    own = jnp.concatenate([block, partner], axis=0)
    forward = lambda s: ((s // 4 + 1) % rings) * 4 + s % 4
    backward = lambda s: ((s // 4 - 1) % rings) * 4 + s % 4
    batches = [[own]]
    ahead, behind = own, own
    for step in range(rings // 2 - 1):
        ahead = moved(ahead, forward)
        behind = moved(behind, backward)
        if step == 0:
            ahead, behind, riders = lax.optimization_barrier((ahead, behind, riders))
        batches[-1] += [ahead, behind]
        if step == 0:
            batches.append([])
    half = own.shape[0] // 2
    batches[-1].append(moved(ahead[:half], forward))
    batches[-1].append(moved(behind[half:], backward))
    mine = [jnp.concatenate(batch, axis=0) for batch in batches]
    other = [moved(chunk, lambda s: s ^ 1) for chunk in mine]
    return mine + other, riders


def normalize(frames, norm_gain):
    widened = frames.astype(jnp.float32)
    inverse = lax.rsqrt(jnp.mean(widened * widened, axis=-1, keepdims=True) + EPSILON)
    return (widened * inverse * norm_gain.astype(jnp.float32)).astype(jnp.bfloat16)


def project(rows, weight, bias):
    return (
        jnp.dot(rows, weight, preferred_element_type=jnp.float32) + bias.astype(jnp.float32)
    ).astype(jnp.bfloat16)


def attend(running, queries, key_rows, value_rows):
    best, mass, total_sum = running
    scores = lax.dot_general(
        queries, key_rows, (((1,), (1,)), ((), ())), preferred_element_type=jnp.float32
    ) * queries.shape[1] ** (-0.5)
    new_best = jnp.maximum(best, jnp.max(scores, axis=1, keepdims=True))
    correction = jnp.exp(best - new_best)
    weights = jnp.exp(scores - new_best)
    mass = mass * correction + jnp.sum(weights, axis=1, keepdims=True)
    total_sum = total_sum * correction + jnp.dot(
        weights.astype(jnp.bfloat16), value_rows, preferred_element_type=jnp.float32
    )
    return (new_best, mass, total_sum)

BLOCK = 768


def attention_kernel(*refs, sizes, channels, resume, finish):
    q_ref, gain_ref, wkv_ref, bkv_ref = refs[:4]
    chunk_refs = refs[4:4 + len(sizes)]
    rest = refs[4 + len(sizes):]
    queries = q_ref[...]
    gain = gain_ref[...]
    wkv = wkv_ref[...]
    bkv = bkv_ref[...]
    count = queries.shape[0]
    if resume:
        best, mass, total = rest[0][...], rest[1][...], rest[2][...]
        rest = rest[3:]
    else:
        best = jnp.full((count, 1), -jnp.inf, jnp.float32)
        mass = jnp.zeros((count, 1), jnp.float32)
        total = jnp.zeros((count, channels), jnp.float32)
    for chunk_ref, size in zip(chunk_refs, sizes):
        for start in range(0, size, BLOCK):
            rows = chunk_ref[start:min(start + BLOCK, size), :].astype(jnp.float32)
            inverse = lax.rsqrt(jnp.mean(rows * rows, axis=-1, keepdims=True) + EPSILON)
            normed = (rows * inverse * gain).astype(jnp.bfloat16)
            both = (jnp.dot(normed, wkv, preferred_element_type=jnp.float32) + bkv).astype(jnp.bfloat16)
            keys = both[:, :channels]
            values = both[:, channels:]
            scores = lax.dot_general(
                queries, keys, (((1,), (1,)), ((), ())), preferred_element_type=jnp.float32
            ) * channels ** (-0.5)
            new_best = jnp.maximum(best, jnp.max(scores, axis=1, keepdims=True))
            correction = jnp.exp(best - new_best)
            weights = jnp.exp(scores - new_best)
            mass = mass * correction + jnp.sum(weights, axis=1, keepdims=True)
            total = total * correction + jnp.dot(
                weights.astype(jnp.bfloat16), values, preferred_element_type=jnp.float32
            )
            best = new_best
    if finish:
        rest[0][...] = (total / mass).astype(rest[0].dtype)
    else:
        rest[0][...] = best
        rest[1][...] = mass
        rest[2][...] = total


def attention_weights(norm_gain, w_qkv, b_qkv):
    channels = w_qkv.shape[0]
    gain = norm_gain.astype(jnp.float32).reshape(1, channels)
    wkv = w_qkv[:, channels:]
    bkv = b_qkv[channels:].astype(jnp.float32).reshape(1, 2 * channels)
    return gain, wkv, bkv


def fused_attention(queries, chunks, weights, state=None, finish=True):
    channels = queries.shape[1]
    count = queries.shape[0]
    sizes = tuple(c.shape[0] for c in chunks)
    gain, wkv, bkv = weights
    spec = pl.BlockSpec(memory_space=pltpu.MemorySpace.VMEM)
    total_rows = sum(sizes)
    flops = 2 * total_rows * channels * (2 * channels + 2 * count)
    extra = tuple(state) if state is not None else ()
    if finish:
        out_shape = jax.ShapeDtypeStruct(queries.shape, jnp.bfloat16)
        out_specs = spec
    else:
        out_shape = (
            jax.ShapeDtypeStruct((count, 1), jnp.float32),
            jax.ShapeDtypeStruct((count, 1), jnp.float32),
            jax.ShapeDtypeStruct((count, channels), jnp.float32),
        )
        out_specs = (spec, spec, spec)
    return pl.pallas_call(
        functools.partial(
            attention_kernel, sizes=sizes, channels=channels, resume=state is not None, finish=finish
        ),
        out_shape=out_shape,
        in_specs=[spec] * (4 + len(chunks) + len(extra)),
        out_specs=out_specs,
        compiler_params=pltpu.CompilerParams(vmem_limit_bytes=48 * 1024 * 1024),
        cost_estimate=pl.CostEstimate(
            flops=flops,
            transcendentals=total_rows * count,
            bytes_accessed=2 * total_rows * channels + 4 * channels * channels + 4 * queries.size,
        ),
    )(queries, gain, wkv, bkv, *chunks, *extra)


def body(
    frames, cache_in, norm_gain, w_qkv, b_qkv, w_proj, b_proj, w_time, b_time, w_space, b_space
):
    channels = frames.shape[-1]
    rows = frames.shape[1]
    width = frames.shape[2]
    out_channels = w_space.shape[-1]
    row_source = ((0, 1, 1), (1, 1, 2))
    tap_lists = [
        sorted({row_tap for parity in row_source for row_tap in range(3) if parity[row_tap] == offset})
        for offset in range(3)
    ]
    stacked = jnp.concatenate([frames, cache_in], axis=0)
    stacked = with_halo(stacked, (("space", 1),), 1)
    extended = stacked[0].reshape(-1, channels)
    carried = stacked[1:].reshape(2, -1, channels)
    normed = normalize(extended, norm_gain)
    riders = dict(
        queries=project(normed, w_qkv[:, :channels], b_qkv[:channels]),
        weights=attention_weights(norm_gain, w_qkv, b_qkv),
        conv=[
            jnp.concatenate([w_space[row_tap, col_tap] for row_tap in taps for col_tap in range(3)], axis=1)
            for taps in tap_lists
        ],
        b_proj=b_proj.astype(jnp.float32),
        b_time=b_time.astype(jnp.float32),
        b_space=b_space.astype(jnp.float32),
    )
    chunks, riders = gather_space(frames.reshape(-1, channels), riders)
    queries = riders["queries"]
    half = len(chunks) // 2
    state = fused_attention(queries, chunks[:half], riders["weights"], finish=False)
    mixed = fused_attention(queries, chunks[half:], riders["weights"], state=state)
    hidden = (
        extended.astype(jnp.float32)
        + jnp.dot(mixed, w_proj, preferred_element_type=jnp.float32)
        + riders["b_proj"]
    ).astype(jnp.bfloat16)
    position = lax.axis_index("tm")
    near_frame = shifted(hidden, "tm", 1)
    near_frame = jnp.where(position == 0, carried[1], near_frame)
    far_frame = shifted(hidden, "tm", 2)
    far_frame = jnp.where(position == 1, carried[1], far_frame)
    far_frame = jnp.where(position == 0, carried[0], far_frame)
    timed = riders["b_time"] + jnp.dot(
        far_frame, w_time[0], preferred_element_type=jnp.float32
    )
    timed = timed + jnp.dot(near_frame, w_time[1], preferred_element_type=jnp.float32)
    timed = (timed + jnp.dot(hidden, w_time[2], preferred_element_type=jnp.float32)).astype(
        jnp.bfloat16
    )
    paired = jnp.stack([timed[:, :channels], timed[:, channels:]]).reshape(2, rows + 2, width, channels)
    place = lax.axis_index("space")
    line = lax.broadcasted_iota(jnp.int32, (1, rows + 2, 1, 1), 1)
    outside = ((place == 0) & (line == 0)) | ((place == lax.axis_size("space") - 1) & (line == rows + 1))
    padded = jnp.where(outside, jnp.zeros_like(paired), paired)
    products = {}
    for offset in range(3):
        taps = tap_lists[offset]
        lhs = padded[:, offset : offset + rows].reshape(-1, channels)
        both = jnp.dot(lhs, riders["conv"][offset], preferred_element_type=jnp.float32)
        both = both.reshape(2, rows, width, len(taps) * 3, out_channels)
        for index, row_tap in enumerate(taps):
            for col_tap in range(3):
                products[offset, row_tap, col_tap] = both[:, :, :, index * 3 + col_tap]

    def shifted_cols(value, steps):
        if steps < 0:
            return jnp.pad(value, ((0, 0), (0, 0), (1, 0), (0, 0)))[:, :, :width]
        return jnp.pad(value, ((0, 0), (0, 0), (0, 1), (0, 0)))[:, :, 1:]

    bias = riders["b_space"]
    rows_out = []
    for parity in row_source:
        taps = [sum(products[parity[row_tap], row_tap, col_tap] for row_tap in range(3)) for col_tap in range(3)]
        even = bias + shifted_cols(taps[0], -1) + taps[1] + taps[2]
        odd = bias + taps[0] + taps[1] + shifted_cols(taps[2], 1)
        rows_out.append(jnp.stack([even, odd], axis=3).astype(jnp.bfloat16))
    result = jnp.stack(rows_out, axis=2)
    return result.reshape(2, 2 * rows, 2 * width, out_channels)


def solution(mesh):
    return jax.shard_map(
        body,
        mesh=mesh,
        in_specs=(
            P("tm", "space", None, None),
            P(None, "space", None, None),
            P(),
            P(),
            P(),
            P(),
            P(),
            P(),
            P(),
            P(),
            P(),
        ),
        out_specs=P("tm", "space", None, None),
        check_vma=False,
    )
```

```python
import functools

import jax
import jax.numpy as jnp
from jax import lax
from jax.experimental import pallas as pl
from jax.experimental.pallas import tpu as pltpu
from jax.sharding import PartitionSpec as P

EPSILON = 1e-06


def shifted(value, axis, steps):
    count = lax.axis_size(axis)
    leading, last = (max(0, -steps), min(count, count - steps))
    return lax.ppermute(value, axis, [(source, source + steps) for source in range(leading, last)])


def with_halo(block, sides, width):
    for axis, dim in sides:
        count = lax.axis_size(axis)
        forward = [(i, i + 1) for i in range(count - 1)]
        backward = [(target, source) for source, target in forward]
        low = lax.ppermute(
            lax.slice_in_dim(block, block.shape[dim] - width, None, axis=dim), axis, forward
        )
        high = lax.ppermute(lax.slice_in_dim(block, 0, width, axis=dim), axis, backward)
        block = jnp.concatenate([low, block, high], axis=dim)
    return block


def gather_space(block, riders):
    count = lax.axis_size("space")
    rings = count // 4

    def moved(value, target):
        return lax.ppermute(value, "space", [(s, target(s)) for s in range(count)])

    partner = moved(block, lambda s: s ^ 2)
    own = jnp.concatenate([block, partner], axis=0)
    forward = lambda s: ((s // 4 + 1) % rings) * 4 + s % 4
    backward = lambda s: ((s // 4 - 1) % rings) * 4 + s % 4
    batches = [[own]]
    ahead, behind = own, own
    for step in range(rings // 2 - 1):
        ahead = moved(ahead, forward)
        behind = moved(behind, backward)
        if step == 0:
            ahead, behind, riders = lax.optimization_barrier((ahead, behind, riders))
        batches[-1] += [ahead, behind]
        if step == 0:
            batches.append([])
    half = own.shape[0] // 2
    batches[-1].append(moved(ahead[:half], forward))
    batches[-1].append(moved(behind[half:], backward))
    mine = [jnp.concatenate(batch, axis=0) for batch in batches]
    other = [moved(chunk, lambda s: s ^ 1) for chunk in mine]
    return mine + other, riders


def normalize(frames, norm_gain):
    widened = frames.astype(jnp.float32)
    inverse = lax.rsqrt(jnp.mean(widened * widened, axis=-1, keepdims=True) + EPSILON)
    return (widened * inverse * norm_gain.astype(jnp.float32)).astype(jnp.bfloat16)


def project(rows, weight, bias):
    return (
        jnp.dot(rows, weight, preferred_element_type=jnp.float32) + bias.astype(jnp.float32)
    ).astype(jnp.bfloat16)


def attend(running, queries, key_rows, value_rows):
    best, mass, total_sum = running
    scores = lax.dot_general(
        queries, key_rows, (((1,), (1,)), ((), ())), preferred_element_type=jnp.float32
    ) * queries.shape[1] ** (-0.5)
    new_best = jnp.maximum(best, jnp.max(scores, axis=1, keepdims=True))
    correction = jnp.exp(best - new_best)
    weights = jnp.exp(scores - new_best)
    mass = mass * correction + jnp.sum(weights, axis=1, keepdims=True)
    total_sum = total_sum * correction + jnp.dot(
        weights.astype(jnp.bfloat16), value_rows, preferred_element_type=jnp.float32
    )
    return (new_best, mass, total_sum)

BLOCK = 1152


def attention_kernel(*refs, sizes, channels, resume, finish):
    q_ref, gain_ref, wkv_ref, bkv_ref = refs[:4]
    chunk_refs = refs[4:4 + len(sizes)]
    rest = refs[4 + len(sizes):]
    queries = q_ref[...]
    gain = gain_ref[...]
    wkv = wkv_ref[...]
    bkv = bkv_ref[...]
    count = queries.shape[0]
    if resume:
        best, mass, total = rest[0][...], rest[1][...], rest[2][...]
        rest = rest[3:]
    else:
        best = jnp.full((count, 1), -jnp.inf, jnp.float32)
        mass = jnp.zeros((count, 1), jnp.float32)
        total = jnp.zeros((count, channels), jnp.float32)
    for chunk_ref, size in zip(chunk_refs, sizes):
        pieces = -(-size // BLOCK)
        step = size // pieces
        for start in range(0, size, step):
            rows = chunk_ref[start:start + step, :].astype(jnp.float32)
            inverse = lax.rsqrt(jnp.mean(rows * rows, axis=-1, keepdims=True) + EPSILON)
            normed = (rows * inverse * gain).astype(jnp.bfloat16)
            both = (jnp.dot(normed, wkv, preferred_element_type=jnp.float32) + bkv).astype(jnp.bfloat16)
            keys = both[:, :channels]
            values = both[:, channels:]
            scores = lax.dot_general(
                queries, keys, (((1,), (1,)), ((), ())), preferred_element_type=jnp.float32
            ) * channels ** (-0.5)
            new_best = jnp.maximum(best, jnp.max(scores, axis=1, keepdims=True))
            correction = jnp.exp(best - new_best)
            weights = jnp.exp(scores - new_best)
            mass = mass * correction + jnp.sum(weights, axis=1, keepdims=True)
            total = total * correction + jnp.dot(
                weights.astype(jnp.bfloat16), values, preferred_element_type=jnp.float32
            )
            best = new_best
    if finish:
        rest[0][...] = (total / mass).astype(rest[0].dtype)
    else:
        rest[0][...] = best
        rest[1][...] = mass
        rest[2][...] = total


def attention_weights(norm_gain, w_qkv, b_qkv):
    channels = w_qkv.shape[0]
    gain = norm_gain.astype(jnp.float32).reshape(1, channels)
    wkv = w_qkv[:, channels:]
    bkv = b_qkv[channels:].astype(jnp.float32).reshape(1, 2 * channels)
    return gain, wkv, bkv


def fused_attention(queries, chunks, weights, state=None, finish=True):
    channels = queries.shape[1]
    count = queries.shape[0]
    sizes = tuple(c.shape[0] for c in chunks)
    gain, wkv, bkv = weights
    spec = pl.BlockSpec(memory_space=pltpu.MemorySpace.VMEM)
    total_rows = sum(sizes)
    flops = 2 * total_rows * channels * (2 * channels + 2 * count)
    extra = tuple(state) if state is not None else ()
    if finish:
        out_shape = jax.ShapeDtypeStruct(queries.shape, jnp.bfloat16)
        out_specs = spec
    else:
        out_shape = (
            jax.ShapeDtypeStruct((count, 1), jnp.float32),
            jax.ShapeDtypeStruct((count, 1), jnp.float32),
            jax.ShapeDtypeStruct((count, channels), jnp.float32),
        )
        out_specs = (spec, spec, spec)
    return pl.pallas_call(
        functools.partial(
            attention_kernel, sizes=sizes, channels=channels, resume=state is not None, finish=finish
        ),
        out_shape=out_shape,
        in_specs=[spec] * (4 + len(chunks) + len(extra)),
        out_specs=out_specs,
        compiler_params=pltpu.CompilerParams(vmem_limit_bytes=48 * 1024 * 1024),
        cost_estimate=pl.CostEstimate(
            flops=flops,
            transcendentals=total_rows * count,
            bytes_accessed=2 * total_rows * channels + 4 * channels * channels + 4 * queries.size,
        ),
    )(queries, gain, wkv, bkv, *chunks, *extra)


def body(
    frames, cache_in, norm_gain, w_qkv, b_qkv, w_proj, b_proj, w_time, b_time, w_space, b_space
):
    channels = frames.shape[-1]
    rows = frames.shape[1]
    width = frames.shape[2]
    out_channels = w_space.shape[-1]
    row_source = ((0, 1, 1), (1, 1, 2))
    tap_lists = [
        sorted({row_tap for parity in row_source for row_tap in range(3) if parity[row_tap] == offset})
        for offset in range(3)
    ]
    normed = normalize(frames, norm_gain).reshape(-1, channels)
    riders = dict(
        queries=project(normed, w_qkv[:, :channels], b_qkv[:channels]),
        weights=attention_weights(norm_gain, w_qkv, b_qkv),
        conv=[
            jnp.concatenate([w_space[row_tap, col_tap] for row_tap in taps for col_tap in range(3)], axis=1)
            for taps in tap_lists
        ],
        b_proj=b_proj.astype(jnp.float32),
        b_time=b_time.astype(jnp.float32),
        b_space=b_space.astype(jnp.float32),
    )
    chunks, riders = gather_space(frames.reshape(-1, channels), riders)
    queries = riders["queries"]
    half = len(chunks) // 2
    state = fused_attention(queries, chunks[:half], riders["weights"], finish=False)
    mixed = fused_attention(queries, chunks[half:], riders["weights"], state=state)
    hidden = (
        frames.reshape(-1, channels).astype(jnp.float32)
        + jnp.dot(mixed, w_proj, preferred_element_type=jnp.float32)
        + riders["b_proj"]
    ).astype(jnp.bfloat16)
    position = lax.axis_index("tm")
    carried = cache_in.reshape(2, -1, channels)
    near_frame = shifted(hidden, "tm", 1)
    near_frame = jnp.where(position == 0, carried[1], near_frame)
    far_frame = shifted(hidden, "tm", 2)
    far_frame = jnp.where(position == 1, carried[1], far_frame)
    far_frame = jnp.where(position == 0, carried[0], far_frame)
    timed = riders["b_time"] + jnp.dot(
        far_frame, w_time[0], preferred_element_type=jnp.float32
    )
    timed = timed + jnp.dot(near_frame, w_time[1], preferred_element_type=jnp.float32)
    timed = (timed + jnp.dot(hidden, w_time[2], preferred_element_type=jnp.float32)).astype(
        jnp.bfloat16
    )
    paired = jnp.stack([timed[:, :channels], timed[:, channels:]]).reshape(2, rows, width, channels)
    padded = with_halo(paired, (("space", 1),), 1)
    products = {}
    for offset in range(3):
        taps = tap_lists[offset]
        lhs = padded[:, offset : offset + rows].reshape(-1, channels)
        both = jnp.dot(lhs, riders["conv"][offset], preferred_element_type=jnp.float32)
        both = both.reshape(2, rows, width, len(taps) * 3, out_channels)
        for index, row_tap in enumerate(taps):
            for col_tap in range(3):
                products[offset, row_tap, col_tap] = both[:, :, :, index * 3 + col_tap]

    def shifted_cols(value, steps):
        if steps < 0:
            return jnp.pad(value, ((0, 0), (0, 0), (1, 0), (0, 0)))[:, :, :width]
        return jnp.pad(value, ((0, 0), (0, 0), (0, 1), (0, 0)))[:, :, 1:]

    bias = riders["b_space"]
    rows_out = []
    for parity in row_source:
        taps = [sum(products[parity[row_tap], row_tap, col_tap] for row_tap in range(3)) for col_tap in range(3)]
        even = bias + shifted_cols(taps[0], -1) + taps[1] + taps[2]
        odd = bias + taps[0] + taps[1] + shifted_cols(taps[2], 1)
        rows_out.append(jnp.stack([even, odd], axis=3).astype(jnp.bfloat16))
    result = jnp.stack(rows_out, axis=2)
    return result.reshape(2, 2 * rows, 2 * width, out_channels)


def solution(mesh):
    return jax.shard_map(
        body,
        mesh=mesh,
        in_specs=(
            P("tm", "space", None, None),
            P(None, "space", None, None),
            P(),
            P(),
            P(),
            P(),
            P(),
            P(),
            P(),
            P(),
            P(),
        ),
        out_specs=P("tm", "space", None, None),
        check_vma=False,
    )
```

```python
import functools

import jax
import jax.numpy as jnp
from jax import lax
from jax.experimental import pallas as pl
from jax.experimental.pallas import tpu as pltpu
from jax.sharding import PartitionSpec as P

EPSILON = 1e-06


def shifted(value, axis, steps):
    count = lax.axis_size(axis)
    leading, last = (max(0, -steps), min(count, count - steps))
    return lax.ppermute(value, axis, [(source, source + steps) for source in range(leading, last)])


def with_halo(block, sides, width):
    for axis, dim in sides:
        count = lax.axis_size(axis)
        forward = [(i, i + 1) for i in range(count - 1)]
        backward = [(target, source) for source, target in forward]
        low = lax.ppermute(
            lax.slice_in_dim(block, block.shape[dim] - width, None, axis=dim), axis, forward
        )
        high = lax.ppermute(lax.slice_in_dim(block, 0, width, axis=dim), axis, backward)
        block = jnp.concatenate([low, block, high], axis=dim)
    return block


def gather_space(block, riders):
    count = lax.axis_size("space")
    rings = count // 4

    def moved(value, target):
        return lax.ppermute(value, "space", [(s, target(s)) for s in range(count)])

    partner = moved(block, lambda s: s ^ 2)
    own = jnp.concatenate([block, partner], axis=0)
    forward = lambda s: ((s // 4 + 1) % rings) * 4 + s % 4
    backward = lambda s: ((s // 4 - 1) % rings) * 4 + s % 4
    batches = [[own]]
    ahead, behind = own, own
    for step in range(rings // 2 - 1):
        ahead = moved(ahead, forward)
        behind = moved(behind, backward)
        if step == 0:
            ahead, behind, riders = lax.optimization_barrier((ahead, behind, riders))
        batches[-1] += [ahead, behind]
        if step == 0:
            batches.append([])
    half = own.shape[0] // 2
    batches[-1].append(moved(ahead[:half], forward))
    batches[-1].append(moved(behind[half:], backward))
    mine = [jnp.concatenate(batch, axis=0) for batch in batches]
    other = [moved(chunk, lambda s: s ^ 1) for chunk in mine]
    return mine + other, riders


def normalize(frames, norm_gain):
    widened = frames.astype(jnp.float32)
    inverse = lax.rsqrt(jnp.mean(widened * widened, axis=-1, keepdims=True) + EPSILON)
    return (widened * inverse * norm_gain.astype(jnp.float32)).astype(jnp.bfloat16)


def project(rows, weight, bias):
    return (
        jnp.dot(rows, weight, preferred_element_type=jnp.float32) + bias.astype(jnp.float32)
    ).astype(jnp.bfloat16)


def attend(running, queries, key_rows, value_rows):
    best, mass, total_sum = running
    scores = lax.dot_general(
        queries, key_rows, (((1,), (1,)), ((), ())), preferred_element_type=jnp.float32
    ) * queries.shape[1] ** (-0.5)
    new_best = jnp.maximum(best, jnp.max(scores, axis=1, keepdims=True))
    correction = jnp.exp(best - new_best)
    weights = jnp.exp(scores - new_best)
    mass = mass * correction + jnp.sum(weights, axis=1, keepdims=True)
    total_sum = total_sum * correction + jnp.dot(
        weights.astype(jnp.bfloat16), value_rows, preferred_element_type=jnp.float32
    )
    return (new_best, mass, total_sum)

BLOCK = 1920


def attention_kernel(*refs, sizes, channels, resume, finish):
    q_ref, gain_ref, wkv_ref, bkv_ref = refs[:4]
    chunk_refs = refs[4:4 + len(sizes)]
    rest = refs[4 + len(sizes):]
    queries = q_ref[...]
    gain = gain_ref[...]
    wkv = wkv_ref[...]
    bkv = bkv_ref[...]
    count = queries.shape[0]
    if resume:
        best, mass, total = rest[0][...], rest[1][...], rest[2][...]
        rest = rest[3:]
    else:
        best = jnp.full((count, 1), -jnp.inf, jnp.float32)
        mass = jnp.zeros((count, 1), jnp.float32)
        total = jnp.zeros((count, channels), jnp.float32)
    for chunk_ref, size in zip(chunk_refs, sizes):
        pieces = -(-size // BLOCK)
        step = size // pieces
        for start in range(0, size, step):
            rows = chunk_ref[start:start + step, :].astype(jnp.float32)
            inverse = lax.rsqrt(jnp.mean(rows * rows, axis=-1, keepdims=True) + EPSILON)
            normed = (rows * inverse * gain).astype(jnp.bfloat16)
            both = (jnp.dot(normed, wkv, preferred_element_type=jnp.float32) + bkv).astype(jnp.bfloat16)
            keys = both[:, :channels]
            values = both[:, channels:]
            scores = lax.dot_general(
                queries, keys, (((1,), (1,)), ((), ())), preferred_element_type=jnp.float32
            ) * channels ** (-0.5)
            new_best = jnp.maximum(best, jnp.max(scores, axis=1, keepdims=True))
            correction = jnp.exp(best - new_best)
            weights = jnp.exp(scores - new_best)
            mass = mass * correction + jnp.sum(weights, axis=1, keepdims=True)
            total = total * correction + jnp.dot(
                weights.astype(jnp.bfloat16), values, preferred_element_type=jnp.float32
            )
            best = new_best
    if finish:
        rest[0][...] = (total / mass).astype(rest[0].dtype)
    else:
        rest[0][...] = best
        rest[1][...] = mass
        rest[2][...] = total


def attention_weights(norm_gain, w_qkv, b_qkv):
    channels = w_qkv.shape[0]
    gain = norm_gain.astype(jnp.float32).reshape(1, channels)
    wkv = w_qkv[:, channels:]
    bkv = b_qkv[channels:].astype(jnp.float32).reshape(1, 2 * channels)
    return gain, wkv, bkv


def fused_attention(queries, chunks, weights, state=None, finish=True):
    channels = queries.shape[1]
    count = queries.shape[0]
    sizes = tuple(c.shape[0] for c in chunks)
    gain, wkv, bkv = weights
    spec = pl.BlockSpec(memory_space=pltpu.MemorySpace.VMEM)
    total_rows = sum(sizes)
    flops = 2 * total_rows * channels * (2 * channels + 2 * count)
    extra = tuple(state) if state is not None else ()
    if finish:
        out_shape = jax.ShapeDtypeStruct(queries.shape, jnp.bfloat16)
        out_specs = spec
    else:
        out_shape = (
            jax.ShapeDtypeStruct((count, 1), jnp.float32),
            jax.ShapeDtypeStruct((count, 1), jnp.float32),
            jax.ShapeDtypeStruct((count, channels), jnp.float32),
        )
        out_specs = (spec, spec, spec)
    return pl.pallas_call(
        functools.partial(
            attention_kernel, sizes=sizes, channels=channels, resume=state is not None, finish=finish
        ),
        out_shape=out_shape,
        in_specs=[spec] * (4 + len(chunks) + len(extra)),
        out_specs=out_specs,
        compiler_params=pltpu.CompilerParams(vmem_limit_bytes=48 * 1024 * 1024),
        cost_estimate=pl.CostEstimate(
            flops=flops,
            transcendentals=total_rows * count,
            bytes_accessed=2 * total_rows * channels + 4 * channels * channels + 4 * queries.size,
        ),
    )(queries, gain, wkv, bkv, *chunks, *extra)


def body(
    frames, cache_in, norm_gain, w_qkv, b_qkv, w_proj, b_proj, w_time, b_time, w_space, b_space
):
    channels = frames.shape[-1]
    rows = frames.shape[1]
    width = frames.shape[2]
    out_channels = w_space.shape[-1]
    row_source = ((0, 1, 1), (1, 1, 2))
    tap_lists = [
        sorted({row_tap for parity in row_source for row_tap in range(3) if parity[row_tap] == offset})
        for offset in range(3)
    ]
    normed = normalize(frames, norm_gain).reshape(-1, channels)
    riders = dict(
        queries=project(normed, w_qkv[:, :channels], b_qkv[:channels]),
        weights=attention_weights(norm_gain, w_qkv, b_qkv),
        conv=[
            jnp.concatenate([w_space[row_tap, col_tap] for row_tap in taps for col_tap in range(3)], axis=1)
            for taps in tap_lists
        ],
        b_proj=b_proj.astype(jnp.float32),
        b_time=b_time.astype(jnp.float32),
        b_space=b_space.astype(jnp.float32),
    )
    chunks, riders = gather_space(frames.reshape(-1, channels), riders)
    queries = riders["queries"]
    half = len(chunks) // 2
    state = fused_attention(queries, chunks[:half], riders["weights"], finish=False)
    mixed = fused_attention(queries, chunks[half:], riders["weights"], state=state)
    hidden = (
        frames.reshape(-1, channels).astype(jnp.float32)
        + jnp.dot(mixed, w_proj, preferred_element_type=jnp.float32)
        + riders["b_proj"]
    ).astype(jnp.bfloat16)
    position = lax.axis_index("tm")
    carried = cache_in.reshape(2, -1, channels)
    near_frame = shifted(hidden, "tm", 1)
    near_frame = jnp.where(position == 0, carried[1], near_frame)
    far_frame = shifted(hidden, "tm", 2)
    far_frame = jnp.where(position == 1, carried[1], far_frame)
    far_frame = jnp.where(position == 0, carried[0], far_frame)
    timed = riders["b_time"] + jnp.dot(
        far_frame, w_time[0], preferred_element_type=jnp.float32
    )
    timed = timed + jnp.dot(near_frame, w_time[1], preferred_element_type=jnp.float32)
    timed = (timed + jnp.dot(hidden, w_time[2], preferred_element_type=jnp.float32)).astype(
        jnp.bfloat16
    )
    paired = jnp.stack([timed[:, :channels], timed[:, channels:]]).reshape(2, rows, width, channels)
    padded = with_halo(paired, (("space", 1),), 1)
    products = {}
    for offset in range(3):
        taps = tap_lists[offset]
        lhs = padded[:, offset : offset + rows].reshape(-1, channels)
        both = jnp.dot(lhs, riders["conv"][offset], preferred_element_type=jnp.float32)
        both = both.reshape(2, rows, width, len(taps) * 3, out_channels)
        for index, row_tap in enumerate(taps):
            for col_tap in range(3):
                products[offset, row_tap, col_tap] = both[:, :, :, index * 3 + col_tap]

    def shifted_cols(value, steps):
        if steps < 0:
            return jnp.pad(value, ((0, 0), (0, 0), (1, 0), (0, 0)))[:, :, :width]
        return jnp.pad(value, ((0, 0), (0, 0), (0, 1), (0, 0)))[:, :, 1:]

    bias = riders["b_space"]
    rows_out = []
    for parity in row_source:
        taps = [sum(products[parity[row_tap], row_tap, col_tap] for row_tap in range(3)) for col_tap in range(3)]
        even = bias + shifted_cols(taps[0], -1) + taps[1] + taps[2]
        odd = bias + taps[0] + taps[1] + shifted_cols(taps[2], 1)
        rows_out.append(jnp.stack([even, odd], axis=3).astype(jnp.bfloat16))
    result = jnp.stack(rows_out, axis=2)
    return result.reshape(2, 2 * rows, 2 * width, out_channels)


def solution(mesh):
    return jax.shard_map(
        body,
        mesh=mesh,
        in_specs=(
            P("tm", "space", None, None),
            P(None, "space", None, None),
            P(),
            P(),
            P(),
            P(),
            P(),
            P(),
            P(),
            P(),
            P(),
        ),
        out_specs=P("tm", "space", None, None),
        check_vma=False,
    )
```

```python
import functools

import jax
import jax.numpy as jnp
from jax import lax
from jax.experimental import pallas as pl
from jax.experimental.pallas import tpu as pltpu
from jax.sharding import PartitionSpec as P

EPSILON = 1e-06


def shifted(value, axis, steps):
    count = lax.axis_size(axis)
    leading, last = (max(0, -steps), min(count, count - steps))
    return lax.ppermute(value, axis, [(source, source + steps) for source in range(leading, last)])


def with_halo(block, sides, width):
    for axis, dim in sides:
        count = lax.axis_size(axis)
        forward = [(i, i + 1) for i in range(count - 1)]
        backward = [(target, source) for source, target in forward]
        low = lax.ppermute(
            lax.slice_in_dim(block, block.shape[dim] - width, None, axis=dim), axis, forward
        )
        high = lax.ppermute(lax.slice_in_dim(block, 0, width, axis=dim), axis, backward)
        block = jnp.concatenate([low, block, high], axis=dim)
    return block


def gather_space(block, riders):
    count = lax.axis_size("space")
    rings = count // 4

    def moved(value, target):
        return lax.ppermute(value, "space", [(s, target(s)) for s in range(count)])

    partner = moved(block, lambda s: s ^ 2)
    own = jnp.concatenate([block, partner], axis=0)
    forward = lambda s: ((s // 4 + 1) % rings) * 4 + s % 4
    backward = lambda s: ((s // 4 - 1) % rings) * 4 + s % 4
    batches = [[own]]
    ahead, behind = own, own
    for step in range(rings // 2 - 1):
        ahead = moved(ahead, forward)
        behind = moved(behind, backward)
        if step == 0:
            ahead, behind, riders = lax.optimization_barrier((ahead, behind, riders))
        batches[-1] += [ahead, behind]
        if step == 0:
            batches.append([])
    half = own.shape[0] // 2
    batches[-1].append(moved(ahead[:half], forward))
    batches[-1].append(moved(behind[half:], backward))
    mine = [jnp.concatenate(batch, axis=0) for batch in batches]
    other = [moved(chunk, lambda s: s ^ 1) for chunk in mine]
    return mine + other, riders


def normalize(frames, norm_gain):
    widened = frames.astype(jnp.float32)
    inverse = lax.rsqrt(jnp.mean(widened * widened, axis=-1, keepdims=True) + EPSILON)
    return (widened * inverse * norm_gain.astype(jnp.float32)).astype(jnp.bfloat16)


def project(rows, weight, bias):
    return (
        jnp.dot(rows, weight, preferred_element_type=jnp.float32) + bias.astype(jnp.float32)
    ).astype(jnp.bfloat16)


def attend(running, queries, key_rows, value_rows):
    best, mass, total_sum = running
    scores = lax.dot_general(
        queries, key_rows, (((1,), (1,)), ((), ())), preferred_element_type=jnp.float32
    ) * queries.shape[1] ** (-0.5)
    new_best = jnp.maximum(best, jnp.max(scores, axis=1, keepdims=True))
    correction = jnp.exp(best - new_best)
    weights = jnp.exp(scores - new_best)
    mass = mass * correction + jnp.sum(weights, axis=1, keepdims=True)
    total_sum = total_sum * correction + jnp.dot(
        weights.astype(jnp.bfloat16), value_rows, preferred_element_type=jnp.float32
    )
    return (new_best, mass, total_sum)

BLOCK = 1920


def attention_kernel(*refs, sizes, channels, resume, finish):
    q_ref, gain_ref, wkv_ref, bkv_ref = refs[:4]
    chunk_refs = refs[4:4 + len(sizes)]
    rest = refs[4 + len(sizes):]
    queries = q_ref[...]
    gain = gain_ref[...]
    wkv = wkv_ref[...]
    bkv = bkv_ref[...]
    count = queries.shape[0]
    if resume:
        best, mass, total = rest[0][...], rest[1][...], rest[2][...]
        rest = rest[3:]
    else:
        best = jnp.full((count, 1), -jnp.inf, jnp.float32)
        mass = jnp.zeros((count, 1), jnp.float32)
        total = jnp.zeros((count, channels), jnp.float32)
    for chunk_ref, size in zip(chunk_refs, sizes):
        pieces = -(-size // BLOCK)
        step = size // pieces
        for start in range(0, size, step):
            rows = chunk_ref[start:start + step, :].astype(jnp.float32)
            inverse = lax.rsqrt(jnp.mean(rows * rows, axis=-1, keepdims=True) + EPSILON)
            normed = (rows * inverse * gain).astype(jnp.bfloat16)
            both = (jnp.dot(normed, wkv, preferred_element_type=jnp.float32) + bkv).astype(jnp.bfloat16)
            keys = both[:, :channels]
            values = both[:, channels:]
            scores = lax.dot_general(
                queries, keys, (((1,), (1,)), ((), ())), preferred_element_type=jnp.float32
            ) * channels ** (-0.5)
            new_best = jnp.maximum(best, jnp.max(scores, axis=1, keepdims=True))
            correction = jnp.exp(best - new_best)
            weights = jnp.exp(scores - new_best)
            mass = mass * correction + jnp.sum(weights, axis=1, keepdims=True)
            total = total * correction + jnp.dot(
                weights.astype(jnp.bfloat16), values, preferred_element_type=jnp.float32
            )
            best = new_best
    if finish:
        rest[0][...] = (total / mass).astype(rest[0].dtype)
    else:
        rest[0][...] = best
        rest[1][...] = mass
        rest[2][...] = total


def attention_weights(norm_gain, w_qkv, b_qkv):
    channels = w_qkv.shape[0]
    gain = norm_gain.astype(jnp.float32).reshape(1, channels)
    wkv = w_qkv[:, channels:]
    bkv = b_qkv[channels:].astype(jnp.float32).reshape(1, 2 * channels)
    return gain, wkv, bkv


def fused_attention(queries, chunks, weights, state=None, finish=True):
    channels = queries.shape[1]
    count = queries.shape[0]
    sizes = tuple(c.shape[0] for c in chunks)
    gain, wkv, bkv = weights
    spec = pl.BlockSpec(memory_space=pltpu.MemorySpace.VMEM)
    total_rows = sum(sizes)
    flops = 2 * total_rows * channels * (2 * channels + 2 * count)
    extra = tuple(state) if state is not None else ()
    if finish:
        out_shape = jax.ShapeDtypeStruct(queries.shape, jnp.bfloat16)
        out_specs = spec
    else:
        out_shape = (
            jax.ShapeDtypeStruct((count, 1), jnp.float32),
            jax.ShapeDtypeStruct((count, 1), jnp.float32),
            jax.ShapeDtypeStruct((count, channels), jnp.float32),
        )
        out_specs = (spec, spec, spec)
    return pl.pallas_call(
        functools.partial(
            attention_kernel, sizes=sizes, channels=channels, resume=state is not None, finish=finish
        ),
        out_shape=out_shape,
        in_specs=[spec] * (4 + len(chunks) + len(extra)),
        out_specs=out_specs,
        compiler_params=pltpu.CompilerParams(vmem_limit_bytes=48 * 1024 * 1024),
        cost_estimate=pl.CostEstimate(
            flops=flops,
            transcendentals=total_rows * count,
            bytes_accessed=2 * total_rows * channels + 4 * channels * channels + 4 * queries.size,
        ),
    )(queries, gain, wkv, bkv, *chunks, *extra)


def body(
    frames, cache_in, norm_gain, w_qkv, b_qkv, w_proj, b_proj, w_time, b_time, w_space, b_space
):
    channels = frames.shape[-1]
    rows = frames.shape[1]
    width = frames.shape[2]
    out_channels = w_space.shape[-1]
    row_source = ((0, 1, 1), (1, 1, 2))
    tap_lists = [
        sorted({row_tap for parity in row_source for row_tap in range(3) if parity[row_tap] == offset})
        for offset in range(3)
    ]
    normed = normalize(frames, norm_gain).reshape(-1, channels)
    riders = dict(
        queries=project(normed, w_qkv[:, :channels], b_qkv[:channels]),
        weights=attention_weights(norm_gain, w_qkv, b_qkv),
        conv=[
            jnp.concatenate([w_space[row_tap, col_tap] for row_tap in taps for col_tap in range(3)], axis=1)
            for taps in tap_lists
        ],
        b_proj=b_proj.astype(jnp.float32),
        b_time=b_time.astype(jnp.float32),
        b_space=b_space.astype(jnp.float32),
    )
    chunks, riders = gather_space(frames.reshape(-1, channels), riders)
    queries = riders["queries"]
    half = len(chunks) // 2
    state = fused_attention(queries, chunks[:half], riders["weights"], finish=False)
    mixed = fused_attention(queries, chunks[half:], riders["weights"], state=state)
    hidden = (
        frames.reshape(-1, channels).astype(jnp.float32)
        + jnp.dot(mixed, w_proj, preferred_element_type=jnp.float32)
        + riders["b_proj"]
    ).astype(jnp.bfloat16)
    position = lax.axis_index("tm")
    carried = cache_in.reshape(2, -1, channels)
    near_frame = shifted(hidden, "tm", 1)
    near_frame = jnp.where(position == 0, carried[1], near_frame)
    far_frame = shifted(hidden, "tm", 2)
    far_frame = jnp.where(position == 1, carried[1], far_frame)
    far_frame = jnp.where(position == 0, carried[0], far_frame)
    timed = riders["b_time"] + jnp.dot(
        far_frame, w_time[0], preferred_element_type=jnp.float32
    )
    timed = timed + jnp.dot(near_frame, w_time[1], preferred_element_type=jnp.float32)
    timed = (timed + jnp.dot(hidden, w_time[2], preferred_element_type=jnp.float32)).astype(
        jnp.bfloat16
    )
    paired = jnp.stack([timed[:, :channels], timed[:, channels:]]).reshape(2, rows, width, channels)
    padded = with_halo(paired, (("space", 1),), 1)
    products = {}
    for offset in range(3):
        taps = tap_lists[offset]
        lhs = padded[:, offset : offset + rows].reshape(-1, channels)
        both = jnp.dot(lhs, riders["conv"][offset], preferred_element_type=jnp.float32)
        both = both.reshape(2, rows, width, len(taps) * 3, out_channels)
        for index, row_tap in enumerate(taps):
            for col_tap in range(3):
                products[offset, row_tap, col_tap] = both[:, :, :, index * 3 + col_tap]

    def shifted_cols(value, steps):
        if steps < 0:
            return jnp.pad(value, ((0, 0), (0, 0), (1, 0), (0, 0)))[:, :, :width]
        return jnp.pad(value, ((0, 0), (0, 0), (0, 1), (0, 0)))[:, :, 1:]

    bias = riders["b_space"]
    rows_out = []
    for parity in row_source:
        taps = [sum(products[parity[row_tap], row_tap, col_tap] for row_tap in range(3)) for col_tap in range(3)]
        even = bias + shifted_cols(taps[0], -1) + taps[1] + taps[2]
        odd = bias + taps[0] + taps[1] + shifted_cols(taps[2], 1)
        rows_out.append(jnp.concatenate([even, odd], axis=-1).astype(jnp.bfloat16))
    result = jnp.stack(rows_out, axis=2)
    return result.reshape(2, 2 * rows, 2 * width, out_channels)


def solution(mesh):
    return jax.shard_map(
        body,
        mesh=mesh,
        in_specs=(
            P("tm", "space", None, None),
            P(None, "space", None, None),
            P(),
            P(),
            P(),
            P(),
            P(),
            P(),
            P(),
            P(),
            P(),
        ),
        out_specs=P("tm", "space", None, None),
        check_vma=False,
    )
```

```python
import functools

import jax
import jax.numpy as jnp
from jax import lax
from jax.experimental import pallas as pl
from jax.experimental.pallas import tpu as pltpu
from jax.sharding import PartitionSpec as P

EPSILON = 1e-06


def shifted(value, axis, steps):
    count = lax.axis_size(axis)
    leading, last = (max(0, -steps), min(count, count - steps))
    return lax.ppermute(value, axis, [(source, source + steps) for source in range(leading, last)])


def with_halo(block, sides, width):
    for axis, dim in sides:
        count = lax.axis_size(axis)
        forward = [(i, i + 1) for i in range(count - 1)]
        backward = [(target, source) for source, target in forward]
        low = lax.ppermute(
            lax.slice_in_dim(block, block.shape[dim] - width, None, axis=dim), axis, forward
        )
        high = lax.ppermute(lax.slice_in_dim(block, 0, width, axis=dim), axis, backward)
        block = jnp.concatenate([low, block, high], axis=dim)
    return block


def gather_space(block, riders):
    count = lax.axis_size("space")
    rings = count // 4

    def moved(value, target):
        return lax.ppermute(value, "space", [(s, target(s)) for s in range(count)])

    partner = moved(block, lambda s: s ^ 2)
    own = jnp.concatenate([block, partner], axis=0)
    forward = lambda s: ((s // 4 + 1) % rings) * 4 + s % 4
    backward = lambda s: ((s // 4 - 1) % rings) * 4 + s % 4
    batches = [[own]]
    ahead, behind = own, own
    for step in range(rings // 2 - 1):
        ahead = moved(ahead, forward)
        behind = moved(behind, backward)
        if step == 0:
            ahead, behind, riders = lax.optimization_barrier((ahead, behind, riders))
        batches[-1] += [ahead, behind]
        if step == 0:
            batches.append([])
    half = own.shape[0] // 2
    batches[-1].append(moved(ahead[:half], forward))
    batches[-1].append(moved(behind[half:], backward))
    mine = [jnp.concatenate(batch, axis=0) for batch in batches]
    other = [moved(chunk, lambda s: s ^ 1) for chunk in mine]
    return mine + other, riders


def normalize(frames, norm_gain):
    widened = frames.astype(jnp.float32)
    inverse = lax.rsqrt(jnp.mean(widened * widened, axis=-1, keepdims=True) + EPSILON)
    return (widened * inverse * norm_gain.astype(jnp.float32)).astype(jnp.bfloat16)


def project(rows, weight, bias):
    return (
        jnp.dot(rows, weight, preferred_element_type=jnp.float32) + bias.astype(jnp.float32)
    ).astype(jnp.bfloat16)


def attend(running, queries, key_rows, value_rows):
    best, mass, total_sum = running
    scores = lax.dot_general(
        queries, key_rows, (((1,), (1,)), ((), ())), preferred_element_type=jnp.float32
    ) * queries.shape[1] ** (-0.5)
    new_best = jnp.maximum(best, jnp.max(scores, axis=1, keepdims=True))
    correction = jnp.exp(best - new_best)
    weights = jnp.exp(scores - new_best)
    mass = mass * correction + jnp.sum(weights, axis=1, keepdims=True)
    total_sum = total_sum * correction + jnp.dot(
        weights.astype(jnp.bfloat16), value_rows, preferred_element_type=jnp.float32
    )
    return (new_best, mass, total_sum)

BLOCK = 1920


def attention_kernel(*refs, sizes, channels, resume, finish):
    q_ref, gain_ref, wkv_ref, bkv_ref = refs[:4]
    chunk_refs = refs[4:4 + len(sizes)]
    rest = refs[4 + len(sizes):]
    queries = q_ref[...]
    gain = gain_ref[...]
    wkv = wkv_ref[...]
    bkv = bkv_ref[...]
    count = queries.shape[0]
    if resume:
        best, mass, total = rest[0][...], rest[1][...], rest[2][...]
        rest = rest[3:]
    else:
        best = jnp.full((count, 1), -jnp.inf, jnp.float32)
        mass = jnp.zeros((count, 1), jnp.float32)
        total = jnp.zeros((count, channels), jnp.float32)
    for chunk_ref, size in zip(chunk_refs, sizes):
        pieces = -(-size // BLOCK)
        step = size // pieces
        for start in range(0, size, step):
            rows = chunk_ref[start:start + step, :].astype(jnp.float32)
            inverse = lax.rsqrt(jnp.mean(rows * rows, axis=-1, keepdims=True) + EPSILON)
            normed = (rows * inverse * gain).astype(jnp.bfloat16)
            both = (jnp.dot(normed, wkv, preferred_element_type=jnp.float32) + bkv).astype(jnp.bfloat16)
            keys = both[:, :channels]
            values = both[:, channels:]
            scores = lax.dot_general(
                queries, keys, (((1,), (1,)), ((), ())), preferred_element_type=jnp.float32
            ) * channels ** (-0.5)
            new_best = jnp.maximum(best, jnp.max(scores, axis=1, keepdims=True))
            correction = jnp.exp(best - new_best)
            weights = jnp.exp(scores - new_best)
            mass = mass * correction + jnp.sum(weights, axis=1, keepdims=True)
            total = total * correction + jnp.dot(
                weights.astype(jnp.bfloat16), values, preferred_element_type=jnp.float32
            )
            best = new_best
    if finish:
        mixed = (total / mass).astype(jnp.bfloat16)
        residual_ref, proj_ref, bproj_ref, out_ref = rest
        out_ref[...] = (
            residual_ref[...].astype(jnp.float32)
            + jnp.dot(mixed, proj_ref[...], preferred_element_type=jnp.float32)
            + bproj_ref[...]
        ).astype(out_ref.dtype)
    else:
        rest[0][...] = best
        rest[1][...] = mass
        rest[2][...] = total


def attention_weights(norm_gain, w_qkv, b_qkv):
    channels = w_qkv.shape[0]
    gain = norm_gain.astype(jnp.float32).reshape(1, channels)
    wkv = w_qkv[:, channels:]
    bkv = b_qkv[channels:].astype(jnp.float32).reshape(1, 2 * channels)
    return gain, wkv, bkv


def fused_attention(queries, chunks, weights, state=None, finish=True, epilogue=()):
    channels = queries.shape[1]
    count = queries.shape[0]
    sizes = tuple(c.shape[0] for c in chunks)
    gain, wkv, bkv = weights
    spec = pl.BlockSpec(memory_space=pltpu.MemorySpace.VMEM)
    total_rows = sum(sizes)
    flops = 2 * total_rows * channels * (2 * channels + 2 * count)
    extra = (tuple(state) if state is not None else ()) + tuple(epilogue)
    if finish:
        out_shape = jax.ShapeDtypeStruct(queries.shape, jnp.bfloat16)
        out_specs = spec
    else:
        out_shape = (
            jax.ShapeDtypeStruct((count, 1), jnp.float32),
            jax.ShapeDtypeStruct((count, 1), jnp.float32),
            jax.ShapeDtypeStruct((count, channels), jnp.float32),
        )
        out_specs = (spec, spec, spec)
    return pl.pallas_call(
        functools.partial(
            attention_kernel, sizes=sizes, channels=channels, resume=state is not None, finish=finish
        ),
        out_shape=out_shape,
        in_specs=[spec] * (4 + len(chunks) + len(extra)),
        out_specs=out_specs,
        compiler_params=pltpu.CompilerParams(vmem_limit_bytes=48 * 1024 * 1024),
        cost_estimate=pl.CostEstimate(
            flops=flops,
            transcendentals=total_rows * count,
            bytes_accessed=2 * total_rows * channels + 4 * channels * channels + 4 * queries.size,
        ),
    )(queries, gain, wkv, bkv, *chunks, *extra)


def body(
    frames, cache_in, norm_gain, w_qkv, b_qkv, w_proj, b_proj, w_time, b_time, w_space, b_space
):
    channels = frames.shape[-1]
    rows = frames.shape[1]
    width = frames.shape[2]
    out_channels = w_space.shape[-1]
    row_source = ((0, 1, 1), (1, 1, 2))
    tap_lists = [
        sorted({row_tap for parity in row_source for row_tap in range(3) if parity[row_tap] == offset})
        for offset in range(3)
    ]
    normed = normalize(frames, norm_gain).reshape(-1, channels)
    riders = dict(
        queries=project(normed, w_qkv[:, :channels], b_qkv[:channels]),
        weights=attention_weights(norm_gain, w_qkv, b_qkv),
        conv=[
            jnp.concatenate([w_space[row_tap, col_tap] for row_tap in taps for col_tap in range(3)], axis=1)
            for taps in tap_lists
        ],
        b_proj=b_proj.astype(jnp.float32),
        b_time=b_time.astype(jnp.float32),
        b_space=b_space.astype(jnp.float32),
    )
    chunks, riders = gather_space(frames.reshape(-1, channels), riders)
    queries = riders["queries"]
    half = len(chunks) // 2
    state = fused_attention(queries, chunks[:half], riders["weights"], finish=False)
    epilogue = (frames.reshape(-1, channels), w_proj, riders["b_proj"].reshape(1, channels))
    hidden = fused_attention(queries, chunks[half:], riders["weights"], state=state, epilogue=epilogue)
    position = lax.axis_index("tm")
    carried = cache_in.reshape(2, -1, channels)
    near_frame = shifted(hidden, "tm", 1)
    near_frame = jnp.where(position == 0, carried[1], near_frame)
    far_frame = shifted(hidden, "tm", 2)
    far_frame = jnp.where(position == 1, carried[1], far_frame)
    far_frame = jnp.where(position == 0, carried[0], far_frame)
    timed = riders["b_time"] + jnp.dot(
        far_frame, w_time[0], preferred_element_type=jnp.float32
    )
    timed = timed + jnp.dot(near_frame, w_time[1], preferred_element_type=jnp.float32)
    timed = (timed + jnp.dot(hidden, w_time[2], preferred_element_type=jnp.float32)).astype(
        jnp.bfloat16
    )
    paired = jnp.stack([timed[:, :channels], timed[:, channels:]]).reshape(2, rows, width, channels)
    padded = with_halo(paired, (("space", 1),), 1)
    products = {}
    for offset in range(3):
        taps = tap_lists[offset]
        lhs = padded[:, offset : offset + rows].reshape(-1, channels)
        both = jnp.dot(lhs, riders["conv"][offset], preferred_element_type=jnp.float32)
        both = both.reshape(2, rows, width, len(taps) * 3, out_channels)
        for index, row_tap in enumerate(taps):
            for col_tap in range(3):
                products[offset, row_tap, col_tap] = both[:, :, :, index * 3 + col_tap]

    def shifted_cols(value, steps):
        if steps < 0:
            return jnp.pad(value, ((0, 0), (0, 0), (1, 0), (0, 0)))[:, :, :width]
        return jnp.pad(value, ((0, 0), (0, 0), (0, 1), (0, 0)))[:, :, 1:]

    bias = riders["b_space"]
    rows_out = []
    for parity in row_source:
        taps = [sum(products[parity[row_tap], row_tap, col_tap] for row_tap in range(3)) for col_tap in range(3)]
        even = bias + shifted_cols(taps[0], -1) + taps[1] + taps[2]
        odd = bias + taps[0] + taps[1] + shifted_cols(taps[2], 1)
        rows_out.append(jnp.concatenate([even, odd], axis=-1).astype(jnp.bfloat16))
    result = jnp.stack(rows_out, axis=2)
    return result.reshape(2, 2 * rows, 2 * width, out_channels)


def solution(mesh):
    return jax.shard_map(
        body,
        mesh=mesh,
        in_specs=(
            P("tm", "space", None, None),
            P(None, "space", None, None),
            P(),
            P(),
            P(),
            P(),
            P(),
            P(),
            P(),
            P(),
            P(),
        ),
        out_specs=P("tm", "space", None, None),
        check_vma=False,
    )
```

```python
import functools

import jax
import jax.numpy as jnp
from jax import lax
from jax.experimental import pallas as pl
from jax.experimental.pallas import tpu as pltpu
from jax.sharding import PartitionSpec as P

EPSILON = 1e-06


def shifted(value, axis, steps):
    count = lax.axis_size(axis)
    leading, last = (max(0, -steps), min(count, count - steps))
    return lax.ppermute(value, axis, [(source, source + steps) for source in range(leading, last)])


def with_halo(block, sides, width):
    for axis, dim in sides:
        count = lax.axis_size(axis)
        forward = [(i, i + 1) for i in range(count - 1)]
        backward = [(target, source) for source, target in forward]
        low = lax.ppermute(
            lax.slice_in_dim(block, block.shape[dim] - width, None, axis=dim), axis, forward
        )
        high = lax.ppermute(lax.slice_in_dim(block, 0, width, axis=dim), axis, backward)
        block = jnp.concatenate([low, block, high], axis=dim)
    return block


def gather_space(block, riders):
    count = lax.axis_size("space")
    rings = count // 4

    def moved(value, target):
        return lax.ppermute(value, "space", [(s, target(s)) for s in range(count)])

    partner = moved(block, lambda s: s ^ 2)
    own = jnp.concatenate([block, partner], axis=0)
    forward = lambda s: ((s // 4 + 1) % rings) * 4 + s % 4
    backward = lambda s: ((s // 4 - 1) % rings) * 4 + s % 4
    batches = [[own]]
    ahead, behind = own, own
    for step in range(rings // 2 - 1):
        ahead = moved(ahead, forward)
        behind = moved(behind, backward)
        if step == 0:
            ahead, behind, riders = lax.optimization_barrier((ahead, behind, riders))
        batches[-1] += [ahead, behind]
        if step == 0:
            batches.append([])
    half = own.shape[0] // 2
    batches[-1].append(moved(ahead[:half], forward))
    batches[-1].append(moved(behind[half:], backward))
    mine = [jnp.concatenate(batch, axis=0) for batch in batches]
    other = [moved(chunk, lambda s: s ^ 1) for chunk in mine]
    return mine + other, riders


def normalize(frames, norm_gain):
    widened = frames.astype(jnp.float32)
    inverse = lax.rsqrt(jnp.mean(widened * widened, axis=-1, keepdims=True) + EPSILON)
    return (widened * inverse * norm_gain.astype(jnp.float32)).astype(jnp.bfloat16)


def project(rows, weight, bias):
    return (
        jnp.dot(rows, weight, preferred_element_type=jnp.float32) + bias.astype(jnp.float32)
    ).astype(jnp.bfloat16)


def attend(running, queries, key_rows, value_rows):
    best, mass, total_sum = running
    scores = lax.dot_general(
        queries, key_rows, (((1,), (1,)), ((), ())), preferred_element_type=jnp.float32
    ) * queries.shape[1] ** (-0.5)
    new_best = jnp.maximum(best, jnp.max(scores, axis=1, keepdims=True))
    correction = jnp.exp(best - new_best)
    weights = jnp.exp(scores - new_best)
    mass = mass * correction + jnp.sum(weights, axis=1, keepdims=True)
    total_sum = total_sum * correction + jnp.dot(
        weights.astype(jnp.bfloat16), value_rows, preferred_element_type=jnp.float32
    )
    return (new_best, mass, total_sum)

BLOCK = 1920


def attention_kernel(*refs, sizes, channels, resume, finish):
    q_ref, gain_ref, wkv_ref, bkv_ref = refs[:4]
    chunk_refs = refs[4:4 + len(sizes)]
    rest = refs[4 + len(sizes):]
    queries = q_ref[...]
    gain = gain_ref[...]
    wkv = wkv_ref[...]
    bkv = bkv_ref[...]
    count = queries.shape[0]
    if resume:
        best, mass, total = rest[0][...], rest[1][...], rest[2][...]
        rest = rest[3:]
    else:
        best = jnp.full((count, 1), -jnp.inf, jnp.float32)
        mass = jnp.zeros((count, 1), jnp.float32)
        total = jnp.zeros((count, channels), jnp.float32)
    for chunk_ref, size in zip(chunk_refs, sizes):
        pieces = -(-size // BLOCK)
        step = size // pieces
        for start in range(0, size, step):
            rows = chunk_ref[start:start + step, :].astype(jnp.float32)
            inverse = lax.rsqrt(jnp.mean(rows * rows, axis=-1, keepdims=True) + EPSILON)
            normed = (rows * inverse * gain).astype(jnp.bfloat16)
            both = (jnp.dot(normed, wkv, preferred_element_type=jnp.float32) + bkv).astype(jnp.bfloat16)
            keys = both[:, :channels]
            values = both[:, channels:]
            scores = lax.dot_general(
                queries, keys, (((1,), (1,)), ((), ())), preferred_element_type=jnp.float32
            ) * channels ** (-0.5)
            new_best = jnp.maximum(best, jnp.max(scores, axis=1, keepdims=True))
            correction = jnp.exp(best - new_best)
            weights = jnp.exp(scores - new_best)
            mass = mass * correction + jnp.sum(weights, axis=1, keepdims=True)
            total = total * correction + jnp.dot(
                weights.astype(jnp.bfloat16), values, preferred_element_type=jnp.float32
            )
            best = new_best
    if finish:
        mixed = (total / mass).astype(jnp.bfloat16)
        residual_ref, proj_ref, bproj_ref, wt_ref, bt_ref, out_ref, part_ref = rest
        hidden = (
            residual_ref[...].astype(jnp.float32)
            + jnp.dot(mixed, proj_ref[...], preferred_element_type=jnp.float32)
            + bproj_ref[...]
        ).astype(out_ref.dtype)
        out_ref[...] = hidden
        part_ref[...] = bt_ref[...] + jnp.dot(hidden, wt_ref[...], preferred_element_type=jnp.float32)
    else:
        rest[0][...] = best
        rest[1][...] = mass
        rest[2][...] = total


def attention_weights(norm_gain, w_qkv, b_qkv):
    channels = w_qkv.shape[0]
    gain = norm_gain.astype(jnp.float32).reshape(1, channels)
    wkv = w_qkv[:, channels:]
    bkv = b_qkv[channels:].astype(jnp.float32).reshape(1, 2 * channels)
    return gain, wkv, bkv


def fused_attention(queries, chunks, weights, state=None, finish=True, epilogue=()):
    channels = queries.shape[1]
    count = queries.shape[0]
    sizes = tuple(c.shape[0] for c in chunks)
    gain, wkv, bkv = weights
    spec = pl.BlockSpec(memory_space=pltpu.MemorySpace.VMEM)
    total_rows = sum(sizes)
    flops = 2 * total_rows * channels * (2 * channels + 2 * count)
    extra = (tuple(state) if state is not None else ()) + tuple(epilogue)
    if finish:
        out_shape = (
            jax.ShapeDtypeStruct(queries.shape, jnp.bfloat16),
            jax.ShapeDtypeStruct((count, 2 * channels), jnp.float32),
        )
        out_specs = (spec, spec)
    else:
        out_shape = (
            jax.ShapeDtypeStruct((count, 1), jnp.float32),
            jax.ShapeDtypeStruct((count, 1), jnp.float32),
            jax.ShapeDtypeStruct((count, channels), jnp.float32),
        )
        out_specs = (spec, spec, spec)
    return pl.pallas_call(
        functools.partial(
            attention_kernel, sizes=sizes, channels=channels, resume=state is not None, finish=finish
        ),
        out_shape=out_shape,
        in_specs=[spec] * (4 + len(chunks) + len(extra)),
        out_specs=out_specs,
        compiler_params=pltpu.CompilerParams(vmem_limit_bytes=48 * 1024 * 1024),
        cost_estimate=pl.CostEstimate(
            flops=flops,
            transcendentals=total_rows * count,
            bytes_accessed=2 * total_rows * channels + 4 * channels * channels + 4 * queries.size,
        ),
    )(queries, gain, wkv, bkv, *chunks, *extra)


def body(
    frames, cache_in, norm_gain, w_qkv, b_qkv, w_proj, b_proj, w_time, b_time, w_space, b_space
):
    channels = frames.shape[-1]
    rows = frames.shape[1]
    width = frames.shape[2]
    out_channels = w_space.shape[-1]
    row_source = ((0, 1, 1), (1, 1, 2))
    tap_lists = [
        sorted({row_tap for parity in row_source for row_tap in range(3) if parity[row_tap] == offset})
        for offset in range(3)
    ]
    normed = normalize(frames, norm_gain).reshape(-1, channels)
    riders = dict(
        queries=project(normed, w_qkv[:, :channels], b_qkv[:channels]),
        weights=attention_weights(norm_gain, w_qkv, b_qkv),
        conv=[
            jnp.concatenate([w_space[row_tap, col_tap] for row_tap in taps for col_tap in range(3)], axis=1)
            for taps in tap_lists
        ],
        b_proj=b_proj.astype(jnp.float32),
        b_time=b_time.astype(jnp.float32),
        b_space=b_space.astype(jnp.float32),
    )
    chunks, riders = gather_space(frames.reshape(-1, channels), riders)
    queries = riders["queries"]
    half = len(chunks) // 2
    state = fused_attention(queries, chunks[:half], riders["weights"], finish=False)
    epilogue = (
        frames.reshape(-1, channels), w_proj, riders["b_proj"].reshape(1, channels),
        w_time[2], riders["b_time"].reshape(1, 2 * channels),
    )
    hidden, local = fused_attention(queries, chunks[half:], riders["weights"], state=state, epilogue=epilogue)
    position = lax.axis_index("tm")
    carried = cache_in.reshape(2, -1, channels)
    near_frame = shifted(hidden, "tm", 1)
    near_frame = jnp.where(position == 0, carried[1], near_frame)
    far_frame = shifted(hidden, "tm", 2)
    far_frame = jnp.where(position == 1, carried[1], far_frame)
    far_frame = jnp.where(position == 0, carried[0], far_frame)
    timed = local + jnp.dot(far_frame, w_time[0], preferred_element_type=jnp.float32)
    timed = (timed + jnp.dot(near_frame, w_time[1], preferred_element_type=jnp.float32)).astype(
        jnp.bfloat16
    )
    paired = jnp.stack([timed[:, :channels], timed[:, channels:]]).reshape(2, rows, width, channels)
    padded = with_halo(paired, (("space", 1),), 1)
    products = {}
    for offset in range(3):
        taps = tap_lists[offset]
        lhs = padded[:, offset : offset + rows].reshape(-1, channels)
        both = jnp.dot(lhs, riders["conv"][offset], preferred_element_type=jnp.float32)
        both = both.reshape(2, rows, width, len(taps) * 3, out_channels)
        for index, row_tap in enumerate(taps):
            for col_tap in range(3):
                products[offset, row_tap, col_tap] = both[:, :, :, index * 3 + col_tap]

    def shifted_cols(value, steps):
        if steps < 0:
            return jnp.pad(value, ((0, 0), (0, 0), (1, 0), (0, 0)))[:, :, :width]
        return jnp.pad(value, ((0, 0), (0, 0), (0, 1), (0, 0)))[:, :, 1:]

    bias = riders["b_space"]
    rows_out = []
    for parity in row_source:
        taps = [sum(products[parity[row_tap], row_tap, col_tap] for row_tap in range(3)) for col_tap in range(3)]
        even = bias + shifted_cols(taps[0], -1) + taps[1] + taps[2]
        odd = bias + taps[0] + taps[1] + shifted_cols(taps[2], 1)
        rows_out.append(jnp.concatenate([even, odd], axis=-1).astype(jnp.bfloat16))
    result = jnp.stack(rows_out, axis=2)
    return result.reshape(2, 2 * rows, 2 * width, out_channels)


def solution(mesh):
    return jax.shard_map(
        body,
        mesh=mesh,
        in_specs=(
            P("tm", "space", None, None),
            P(None, "space", None, None),
            P(),
            P(),
            P(),
            P(),
            P(),
            P(),
            P(),
            P(),
            P(),
        ),
        out_specs=P("tm", "space", None, None),
        check_vma=False,
    )
```
